512 devices in a mesh: ctx: 32 (over z_hi, x, y), exp: 16 (over z_lo, core).
Axes of the slice: x: 4, y: 4, z: 16 (z_hi: 2, z_lo: 8; z = z_hi * 8 + z_lo), core: 2. Of those that a mesh axis runs over, the one named last changes fastest.
Arguments:
- residual: bfloat16 [4096, 4096], P(('ctx', 'exp')), may hold values from -6 to 6
- queries: bfloat16 [4096, 4096], P('ctx', 'exp'), may hold values from -8 to 8
- keys: bfloat16 [4096, 256], P('ctx'), may hold values from -8 to 8
- values: bfloat16 [4096, 256], P('ctx'), may hold values from -6 to 6
- span_pos: int32 [64], replicated, may hold values from 0 to 63, each once
- out_proj: bfloat16 [4096, 4096], P('exp'), may hold values from -0.71875 to 0.71875
- norm_gain: float32 [4096], replicated, may hold values from 0.25 to 1.75
- expert_gate: bfloat16 [16, 4096, 768], P('exp', None, 'ctx'), may hold values from -0.09375 to 0.09375
- expert_up: bfloat16 [16, 4096, 768], P('exp', None, 'ctx'), may hold values from -0.09375 to 0.09375
- expert_ids: int32 [4096, 8], P(('ctx', 'exp')), may hold values from 0 to 15, all different within a row; in each aligned block of 8 rows (0 to 7, 8 to 15, ...) at most 6 rows name the same one
- route_weight: float32 [4096, 8], P(('ctx', 'exp')), may hold values from 0.25 to 2
Outputs:
- mixed: bfloat16 [4096, 4096], P(('ctx', 'exp'))
- routed: bfloat16 [4096, 8, 768], P(('ctx', 'exp'))
The draws below stay inside these ranges and needn't reach their ends.
Inputs may be any that keep to these rules, and one draw needn't show every extreme that they name: `span_pos`: every span number appears once. `expert_ids`: each row names 8 different experts; among the rows of one device (8 rows in a row, aligned) no expert is named more than 6 times, and in some device's rows some expert is named exactly 6 times.
All inputs are finite; a program needn't handle non-finite values.
Results may differ from the reference program's by a relative error of at most 0.035.
Values may be sent and summed in bfloat16 or wider, within the bound.
No kernel may reach another device: no remote copies, remote signals or barrier semaphores. Data moves between devices by JAX's collectives and lax.ppermute only.
A program may use at most 128 MiB of HBM per device.

```python
import math
import jax
import jax.numpy as jnp
import numpy as np
from jax import lax

D = 4096
HQ = 32
KVH = 2
HD = 128
FE = 768
EXPERTS = 16
TOPK = 8
SEQ = 4096
CH = 64
SPANS = 64
TOK_DEV = 8
MOST = 6
QPD = 2
N_EXP = 16


def query_key_pair(key):
    key_q, key_k = jax.random.split(key, 2)
    query_arr = jnp.clip(jax.random.normal(key_q, (SEQ, HQ * HD), jnp.float32), -4.0, 4.0)
    key_arr = jnp.clip(jax.random.normal(key_k, (SEQ, KVH * HD), jnp.float32), -4.0, 4.0)
    return (query_arr, key_arr)


def draw_queries(key, part):
    return query_key_pair(jax.random.fold_in(key, 7))[0].astype(jnp.bfloat16)


def draw_keys(key, part):
    return query_key_pair(jax.random.fold_in(key, 7))[1].astype(jnp.bfloat16)


def steps_of(stream_key, dims, cuts, smallest, top_value):
    def one(dim, parts):
        draws = jax.random.uniform(jax.random.fold_in(jax.random.fold_in(stream_key, 6), dim), (parts,), jnp.float32, smallest / len(cuts), top_value / len(cuts))
        return jnp.repeat(jnp.exp(draws), dims[dim] // parts).reshape((-1,) + (1,) * (len(dims) - dim - 1))

    loudness = one(*cuts[0])
    for cut in cuts[1:]:
        loudness = loudness * one(*cut)
    return loudness


def routed_block(stream_key, own, number, rows, amount, top, most, lean):
    sequence = jax.random.permutation(stream_key, amount)
    heavy_load, ordinary = portions_of(amount, rows * top, most, lean, True), portions_of(amount, rows * top, most, lean, False)
    places = jnp.arange(amount)

    def named(tallies, rotation):
        used = int((tallies > 0).sum())
        fixed = max(1, used // 4)
        passed = fixed + (places - fixed + rotation * (used - fixed)) % max(1, amount - fixed)
        return jnp.zeros((amount,), jnp.int32).at[sequence[jnp.where(places < fixed, places, passed)]].set(jnp.asarray(tallies, jnp.int32))

    tallies = jnp.where(number % 4 == 0, named(heavy_load, number // 4), named(ordinary, number - number // 4 - 1))
    mixed = jax.random.permutation(jax.random.fold_in(own, 3), amount)
    source_of, sink = mixed[0:amount // 2 * 2:2], mixed[1:amount // 2 * 2:2]
    room = jnp.minimum(tallies[source_of] - 1, most - tallies[sink]) // 2
    room = jnp.where((source_of == sequence[0]) | (sink == sequence[0]) | (tallies[sink] == 0), 0, jnp.maximum(room, 0))
    passed = jax.random.randint(jax.random.fold_in(own, 4), (amount // 2,), 0, 1 << 20) % (room + 1)
    tallies = tallies.at[source_of].add(-passed).at[sink].add(passed)
    items = jnp.searchsorted(jnp.cumsum(tallies), jnp.arange(rows * top), side="right").astype(jnp.int32)
    listing = items.reshape(top, rows).T
    listing = listing[jax.random.permutation(jax.random.fold_in(own, 1), rows)]
    rotation = jax.random.randint(jax.random.fold_in(own, 2), (rows, 1), 0, top)
    return jnp.take_along_axis(listing, (jnp.arange(top)[None, :] + rotation) % top, axis=1)


def portions_of(amount, total, bound, skew, full):
    portions = [(1 << 20) // math.isqrt(standing ** skew) + 1 for standing in range(1, amount + 1)]
    largest = bound if full else min(bound, max(-(-total // amount), total * portions[0] // sum(portions)))
    least = 1 if total - largest >= amount - 1 else 0
    holding, surplus = [largest] + [least] * (amount - 1), total - largest - least * (amount - 1)
    while surplus > 0:
        candidates = [i for i in range(1, amount) if holding[i] < largest] or [i for i in range(1, amount) if holding[i] < bound]
        whole, budget = sum([portions[i] for i in candidates]), surplus
        for i in candidates:
            addition = min(bound - holding[i], max(1, budget * portions[i] // whole), surplus)
            holding[i] = holding[i] + addition
            surplus = surplus - addition
    return np.array(holding)


def bell_draw(rng, extent, scale, reach, cuts=(), held_as=jnp.bfloat16):
    entries = jax.random.normal(rng, extent, jnp.float32) * scale
    if len(cuts) > 0:
        entries = steps_of(rng, extent, cuts, -0.22, 0.18) * entries
    return jnp.clip(entries, min=-reach, max=reach).astype(held_as)


def setup_inputs(seed: int = 0) -> dict:
    key_list = jax.random.split(jax.random.key(seed), 12)
    residual = bell_draw(key_list[0], (SEQ, D), 1.0, 6.0, ((0, 512),))
    queries = draw_queries(jax.random.fold_in(key_list[11], 71), 0)
    keys = draw_keys(jax.random.fold_in(key_list[11], 71), 0)
    values = bell_draw(key_list[3], (SEQ, KVH * HD), 1.0, 6.0, ((0, 32),))
    span_pos = jax.random.permutation(key_list[4], SPANS).astype(jnp.int32)
    out_proj = bell_draw(key_list[5], (HQ * HD, D), 0.12, 0.71875, ((0, 16),))
    norm_gain = jnp.clip(1.0 + 0.15 * jax.random.normal(key_list[6], (D,), jnp.float32), 0.25, 1.75)
    expert_gate = bell_draw(key_list[7], (EXPERTS, D, FE), D ** -0.5, 0.09375, ((0, 16), (2, 32)))
    expert_up = bell_draw(key_list[8], (EXPERTS, D, FE), D ** -0.5, 0.09375, ((0, 16), (2, 32)))
    expert_ids_keys = jax.random.split(jax.random.fold_in(key_list[9], 1), SEQ // TOK_DEV)
    expert_ids_turns = jax.random.permutation(jax.random.fold_in(key_list[9], 3), SEQ // TOK_DEV)
    expert_ids = jax.vmap(lambda own, number: routed_block(jax.random.fold_in(key_list[9], 2), own, number, TOK_DEV, EXPERTS, TOPK, MOST, 2))(expert_ids_keys, expert_ids_turns).reshape((SEQ, TOPK))
    route_weight = jnp.clip(jnp.exp(math.log(2.0) - 2.0794415 * jax.random.uniform(key_list[10], (SEQ, TOPK), jnp.float32) ** steps_of(key_list[10], (SEQ, TOPK), ((0, 512),), -0.2, 0.2)), 0.25, 2.0)
    return {"residual": residual, "queries": queries, "keys": keys, "values": values, "span_pos": span_pos, "out_proj": out_proj, "norm_gain": norm_gain, "expert_gate": expert_gate, "expert_up": expert_up, "expert_ids": expert_ids, "route_weight": route_weight}


def positions(span_pos):
    rows = jnp.arange(SEQ, dtype=jnp.int32)
    return (span_pos[rows // CH] * CH + rows % CH).astype(jnp.int32)

def reference(residual, queries, keys, values, span_pos, out_proj, norm_gain, expert_gate, expert_up, expert_ids, route_weight):
    seq_pos = positions(span_pos)
    visible = seq_pos[None, :] <= seq_pos[:, None]
    scale = 1.0 / math.sqrt(HD)
    group = HQ // KVH

    def one_head(head):
        kv_head = head // group
        query = lax.dynamic_slice_in_dim(queries, head * HD, HD, 1)
        key_part = lax.dynamic_slice_in_dim(keys, kv_head * HD, HD, 1)
        value_part = lax.dynamic_slice_in_dim(values, kv_head * HD, HD, 1)
        scores = jnp.dot(query, key_part.T, preferred_element_type=jnp.float32) * scale
        scores = jnp.where(visible, scores, -1e+30)
        top = lax.optimization_barrier(jnp.max(scores, axis=1, keepdims=True))
        probs = jnp.where(visible, jnp.exp(scores - top), 0.0)
        total = lax.optimization_barrier(jnp.sum(probs, axis=1, keepdims=True))
        summed = jnp.dot(probs.astype(jnp.bfloat16), value_part, preferred_element_type=jnp.float32)
        return (summed / total).astype(jnp.bfloat16)
    heads = lax.map(one_head, jnp.arange(HQ, dtype=jnp.int32))
    attn = jnp.transpose(heads, (1, 0, 2)).reshape(SEQ, HQ * HD)
    width = QPD * HD
    head_total = jnp.zeros((SEQ, D), jnp.float32)
    for group_index in range(N_EXP):
        cols = slice(group_index * width, (group_index + 1) * width)
        share = jnp.dot(attn[:, cols], out_proj[cols], preferred_element_type=jnp.float32).astype(jnp.bfloat16)
        share = lax.optimization_barrier(share)
        head_total = head_total + share.astype(jnp.float32)
    mixed = (residual.astype(jnp.float32) + head_total).astype(jnp.bfloat16)
    mixed_f = mixed.astype(jnp.float32)
    square = lax.optimization_barrier(jnp.mean(mixed_f * mixed_f, axis=1, keepdims=True))
    normed = (mixed_f * lax.rsqrt(square + 1e-06) * norm_gain[None, :]).astype(jnp.bfloat16)

    def one_expert(accum, expert):
        gate = jnp.dot(normed, expert_gate[expert], preferred_element_type=jnp.float32)
        upper = jnp.dot(normed, expert_up[expert], preferred_element_type=jnp.float32)
        hidden = jax.nn.silu(gate) * upper
        chosen = expert_ids == expert
        term = route_weight[:, :, None] * hidden[:, None, :]
        return (accum + jnp.where(chosen[:, :, None], term, 0.0), None)
    start_acc = jnp.zeros((SEQ, TOPK, FE), jnp.float32)
    accum, _ = lax.scan(one_expert, start_acc, jnp.arange(EXPERTS, dtype=jnp.int32))
    return (mixed, accum.astype(jnp.bfloat16))
```

```python
import math

import jax
import jax.numpy as jnp
import numpy as np
from jax import lax
from jax.sharding import Mesh
from jax.sharding import PartitionSpec as P

D = 4096
HQ = 32
KVH = 2
HD = 128
FE = 768
EXPERTS = 16
TOPK = 8
CH = 64

CTX = ("zh", "x", "y")
EXP = ("zl", "c")


def stored_positions(span_pos, rows):
    span = rows // CH
    table = span[:, None] == jnp.arange(span_pos.shape[0], dtype=jnp.int32)[None, :]
    base = jnp.sum(jnp.where(table, span_pos[None, :], 0), axis=1)
    return base * CH + rows % CH


def doubling_bits(n):
    bits = []
    b = n // 2
    while b >= 1:
        bits.append(b)
        b //= 2
    return bits


def gather_by_doubling(piece, n):
    idx = lax.axis_index(CTX)
    cur = piece
    order = [0]
    for bit in doubling_bits(n):
        other = lax.ppermute(cur, CTX, [(i, i ^ bit) for i in range(n)])
        low = (idx & bit) == 0
        cur = jnp.where(low, jnp.concatenate([cur, other]), jnp.concatenate([other, cur]))
        order = order + [o + bit for o in order]
    return cur, order


def shards(
    residual,
    queries,
    keys,
    values,
    span_pos,
    out_proj,
    norm_gain,
    expert_gate,
    expert_up,
    expert_ids,
    route_weight,
    n_ctx,
    n_xy,
    n_zh,
):
    tok_rows = queries.shape[0]
    per_device = queries.shape[1] // HD
    group = HQ // KVH
    ctx_index = lax.axis_index(CTX)
    exp_index = lax.axis_index(EXP)
    n_exp = EXPERTS

    fe_dev = expert_gate.shape[2]
    w_local = jnp.concatenate([expert_gate[0].T, expert_up[0].T], axis=0)
    w_all = lax.all_gather(w_local, "zh", axis=0, tiled=True)
    w_all = lax.all_gather(w_all, ("x", "y"), axis=0, tiled=True)

    kv_head = exp_index * per_device // group
    own_keys = lax.dynamic_slice_in_dim(keys, kv_head * HD, HD, 1)
    own_values = lax.dynamic_slice_in_dim(values, kv_head * HD, HD, 1)
    kv_local = jnp.concatenate([own_keys, own_values], axis=1)
    kv_all, order = gather_by_doubling(kv_local, n_ctx)
    key_piece = kv_all[:, :HD]
    value_piece = kv_all[:, HD:]
    length = key_piece.shape[0]
    block_ctx = jnp.asarray(np.array(order, np.int32))
    key_rows_all = (
        jnp.repeat(block_ctx, tok_rows) * tok_rows
        + jnp.tile(jnp.arange(tok_rows, dtype=jnp.int32), n_ctx)
    )

    query_pos = stored_positions(
        span_pos, ctx_index * tok_rows + jnp.arange(tok_rows, dtype=jnp.int32)
    )
    query_heads = queries.reshape(tok_rows, per_device, HD)
    scale = 1.0 / math.sqrt(HD)
    carry = (
        jnp.full((per_device, tok_rows), -1e30, jnp.float32),
        jnp.zeros((per_device, tok_rows), jnp.float32),
        jnp.zeros((per_device, tok_rows, HD), jnp.float32),
    )
    block = min(length, 1024)
    for begin in range(0, length, block):
        stop = min(begin + block, length)
        attend_key_piece = key_piece[begin:stop]
        attend_value_piece = value_piece[begin:stop]
        attend_running, attend_total, attend_accum = carry
        key_pos = stored_positions(span_pos, key_rows_all[begin:stop])
        scores = (
            jnp.einsum(
                "tqd,nd->qtn", query_heads, attend_key_piece, preferred_element_type=jnp.float32
            )
            * scale
        )
        visible = key_pos[None, None, :] <= query_pos[None, :, None]
        block_top = jnp.max(jnp.where(visible, scores, -1e30), axis=2)
        new_top = jnp.maximum(attend_running, block_top)
        factor = jnp.exp(attend_running - new_top)
        probs = jnp.where(visible, jnp.exp(scores - new_top[:, :, None]), 0.0)
        attend_total = attend_total * factor + jnp.sum(probs, axis=2)
        summed = jnp.einsum(
            "qtn,nd->qtd",
            probs.astype(jnp.bfloat16),
            attend_value_piece,
            preferred_element_type=jnp.float32,
        )
        attend_accum = attend_accum * factor[:, :, None] + summed
        carry = (new_top, attend_total, attend_accum)
    running, total, accum = carry
    attn = (accum / total[:, :, None]).astype(jnp.bfloat16)
    attn = jnp.transpose(attn, (1, 0, 2)).reshape(tok_rows, per_device * HD)
    tok_dev = residual.shape[0]

    share = jnp.dot(attn, out_proj, preferred_element_type=jnp.float32).astype(jnp.bfloat16)
    shares = lax.all_to_all(
        share.reshape(n_exp, tok_dev, D), EXP, split_axis=0, concat_axis=0, tiled=True
    )
    head_total = jnp.sum(shares.astype(jnp.float32), axis=0)
    mixed = (residual.astype(jnp.float32) + head_total).astype(jnp.bfloat16)
    mixed_f = mixed.astype(jnp.float32)
    square = jnp.mean(mixed_f * mixed_f, axis=1, keepdims=True)
    normed = (mixed_f * lax.rsqrt(square + 1e-06) * norm_gain[None, :]).astype(jnp.bfloat16)

    most_slots = 3 * tok_dev // 4
    ids_flat = expert_ids.reshape(-1)
    onehot = (ids_flat[:, None] == jnp.arange(EXPERTS, dtype=jnp.int32)[None, :]).astype(jnp.int32)
    earlier = jnp.cumsum(onehot, axis=0) - onehot
    slot = jnp.sum(earlier * onehot, axis=1)
    target = ids_flat * most_slots + slot
    placing = (
        target[:, None] == jnp.arange(EXPERTS * most_slots, dtype=jnp.int32)[None, :]
    ).astype(jnp.bfloat16)
    placing = jnp.sum(placing.reshape(tok_dev, TOPK, EXPERTS * most_slots), axis=1)
    outgoing = jnp.einsum("ts,td->sd", placing, normed, preferred_element_type=jnp.float32).astype(
        jnp.bfloat16
    )
    outgoing = outgoing.reshape(EXPERTS, most_slots, D)
    received = lax.all_to_all(outgoing, EXP, split_axis=0, concat_axis=0, tiled=True)
    received = received.reshape(EXPERTS * most_slots, D)

    proj = jnp.einsum("sd,fd->sf", received, w_all, preferred_element_type=jnp.float32)
    proj = proj.reshape(EXPERTS * most_slots, n_xy, n_zh, 2, fe_dev)
    hidden = jax.nn.silu(proj[:, :, :, 0]) * proj[:, :, :, 1]
    hidden = jnp.transpose(hidden, (0, 2, 1, 3)).reshape(EXPERTS, most_slots, FE)
    returned = (
        lax.all_to_all(hidden.astype(jnp.bfloat16), EXP, split_axis=0, concat_axis=0, tiled=True)
        .astype(jnp.float32)
        .reshape(EXPERTS * most_slots, FE)
    )
    picked = jnp.take(returned, target, axis=0)
    routed = (picked * route_weight.reshape(-1)[:, None]).astype(jnp.bfloat16)
    return (mixed, routed.reshape(tok_dev, TOPK, FE))


def solution(mesh):
    n_ctx = mesh.shape["ctx"]
    n_exp = mesh.shape["exp"]
    n_zh = 2
    n_xy = n_ctx // n_zh
    side = int(round(math.sqrt(n_xy)))
    n_zl = n_exp // 2
    fine = Mesh(mesh.devices.reshape(n_zh, side, n_xy // side, n_zl, 2), CTX + EXP)
    tok = CTX + EXP
    in_specs = (
        P(tok, None),
        P(CTX, EXP),
        P(CTX, None),
        P(CTX, None),
        P(),
        P(EXP, None),
        P(),
        P(EXP, None, CTX),
        P(EXP, None, CTX),
        P(tok, None),
        P(tok, None),
    )
    out_specs = (P(tok, None), P(tok, None, None))

    def body(*args):
        return shards(*args, n_ctx=n_ctx, n_xy=n_xy, n_zh=n_zh)

    return jax.shard_map(body, mesh=fine, in_specs=in_specs, out_specs=out_specs, check_vma=False)
```

```python
import math

import jax
import jax.numpy as jnp
import numpy as np
from jax import lax
from jax.sharding import Mesh
from jax.sharding import PartitionSpec as P

D = 4096
HQ = 32
KVH = 2
HD = 128
FE = 768
EXPERTS = 16
TOPK = 8
CH = 64

CTX = ("zh", "x", "y")
EXP = ("zl", "c")


def stored_positions(span_pos, rows):
    span = rows // CH
    table = span[:, None] == jnp.arange(span_pos.shape[0], dtype=jnp.int32)[None, :]
    base = jnp.sum(jnp.where(table, span_pos[None, :], 0), axis=1)
    return base * CH + rows % CH


def doubling_bits(n):
    bits = []
    b = n // 2
    while b >= 1:
        bits.append(b)
        b //= 2
    return bits


def gather_by_doubling(piece, n):
    idx = lax.axis_index(CTX)
    cur = piece
    order = [0]
    for bit in doubling_bits(n):
        other = lax.ppermute(cur, CTX, [(i, i ^ bit) for i in range(n)])
        low = (idx & bit) == 0
        cur = jnp.where(low, jnp.concatenate([cur, other]), jnp.concatenate([other, cur]))
        order = order + [o + bit for o in order]
    return cur, order


def shards(
    residual,
    queries,
    keys,
    values,
    span_pos,
    out_proj,
    norm_gain,
    expert_gate,
    expert_up,
    expert_ids,
    route_weight,
    n_ctx,
    n_xy,
    n_zh,
):
    tok_rows = queries.shape[0]
    per_device = queries.shape[1] // HD
    group = HQ // KVH
    ctx_index = lax.axis_index(CTX)
    exp_index = lax.axis_index(EXP)
    n_exp = EXPERTS

    fe_dev = expert_gate.shape[2]
    w_local = jnp.concatenate([expert_gate[0].T, expert_up[0].T], axis=0)
    zh_index = lax.axis_index("zh")
    w_other = lax.ppermute(w_local, "zh", [(0, 1), (1, 0)])
    w_pair = jnp.where(
        zh_index == 0,
        jnp.concatenate([w_local, w_other]),
        jnp.concatenate([w_other, w_local]),
    )
    w_all = lax.all_gather(w_pair, ("x", "y"), axis=0, tiled=True)

    kv_head = exp_index * per_device // group
    own_keys = lax.dynamic_slice_in_dim(keys, kv_head * HD, HD, 1)
    own_values = lax.dynamic_slice_in_dim(values, kv_head * HD, HD, 1)
    kv_local = jnp.concatenate([own_keys, own_values], axis=1)
    kv_all, order = gather_by_doubling(kv_local, n_ctx)
    key_piece = kv_all[:, :HD]
    value_piece = kv_all[:, HD:]
    length = key_piece.shape[0]
    block_ctx = jnp.asarray(np.array(order, np.int32))
    key_rows_all = (
        jnp.repeat(block_ctx, tok_rows) * tok_rows
        + jnp.tile(jnp.arange(tok_rows, dtype=jnp.int32), n_ctx)
    )

    query_pos = stored_positions(
        span_pos, ctx_index * tok_rows + jnp.arange(tok_rows, dtype=jnp.int32)
    )
    query_heads = queries.reshape(tok_rows, per_device, HD)
    scale = 1.0 / math.sqrt(HD)
    carry = (
        jnp.full((per_device, tok_rows), -1e30, jnp.float32),
        jnp.zeros((per_device, tok_rows), jnp.float32),
        jnp.zeros((per_device, tok_rows, HD), jnp.float32),
    )
    block = min(length, 1024)
    for begin in range(0, length, block):
        stop = min(begin + block, length)
        attend_key_piece = key_piece[begin:stop]
        attend_value_piece = value_piece[begin:stop]
        attend_running, attend_total, attend_accum = carry
        key_pos = stored_positions(span_pos, key_rows_all[begin:stop])
        scores = (
            jnp.einsum(
                "tqd,nd->qtn", query_heads, attend_key_piece, preferred_element_type=jnp.float32
            )
            * scale
        )
        visible = key_pos[None, None, :] <= query_pos[None, :, None]
        block_top = jnp.max(jnp.where(visible, scores, -1e30), axis=2)
        new_top = jnp.maximum(attend_running, block_top)
        factor = jnp.exp(attend_running - new_top)
        probs = jnp.where(visible, jnp.exp(scores - new_top[:, :, None]), 0.0)
        attend_total = attend_total * factor + jnp.sum(probs, axis=2)
        summed = jnp.einsum(
            "qtn,nd->qtd",
            probs.astype(jnp.bfloat16),
            attend_value_piece,
            preferred_element_type=jnp.float32,
        )
        attend_accum = attend_accum * factor[:, :, None] + summed
        carry = (new_top, attend_total, attend_accum)
    running, total, accum = carry
    attn = (accum / total[:, :, None]).astype(jnp.bfloat16)
    attn = jnp.transpose(attn, (1, 0, 2)).reshape(tok_rows, per_device * HD)
    tok_dev = residual.shape[0]

    share = jnp.dot(attn, out_proj, preferred_element_type=jnp.float32).astype(jnp.bfloat16)
    core_index = lax.axis_index("c")
    by_core = jnp.transpose(share.reshape(n_exp // 2, 2, tok_dev, D), (1, 0, 2, 3))
    keep = jnp.where(core_index == 0, by_core[0], by_core[1])
    give = jnp.where(core_index == 0, by_core[1], by_core[0])
    got = lax.ppermute(give, "c", [(0, 1), (1, 0)])
    pair_sum = (keep.astype(jnp.float32) + got.astype(jnp.float32)).astype(jnp.bfloat16)
    shares = lax.all_to_all(pair_sum, "zl", split_axis=0, concat_axis=0, tiled=True)
    head_total = jnp.sum(shares.astype(jnp.float32), axis=0)
    mixed = (residual.astype(jnp.float32) + head_total).astype(jnp.bfloat16)
    mixed_f = mixed.astype(jnp.float32)
    square = jnp.mean(mixed_f * mixed_f, axis=1, keepdims=True)
    normed = (mixed_f * lax.rsqrt(square + 1e-06) * norm_gain[None, :]).astype(jnp.bfloat16)

    most_slots = 3 * tok_dev // 4
    ids_flat = expert_ids.reshape(-1)
    onehot = (ids_flat[:, None] == jnp.arange(EXPERTS, dtype=jnp.int32)[None, :]).astype(jnp.int32)
    earlier = jnp.cumsum(onehot, axis=0) - onehot
    slot = jnp.sum(earlier * onehot, axis=1)
    target = ids_flat * most_slots + slot
    placing = (
        target[:, None] == jnp.arange(EXPERTS * most_slots, dtype=jnp.int32)[None, :]
    ).astype(jnp.bfloat16)
    placing = jnp.sum(placing.reshape(tok_dev, TOPK, EXPERTS * most_slots), axis=1)
    outgoing = jnp.einsum("ts,td->sd", placing, normed, preferred_element_type=jnp.float32).astype(
        jnp.bfloat16
    )
    outgoing = outgoing.reshape(EXPERTS, most_slots, D)
    received = lax.all_to_all(outgoing, EXP, split_axis=0, concat_axis=0, tiled=True)
    received = received.reshape(EXPERTS * most_slots, D)

    proj = jnp.einsum("sd,fd->sf", received, w_all, preferred_element_type=jnp.float32)
    proj = proj.reshape(EXPERTS * most_slots, n_xy, n_zh, 2, fe_dev)
    hidden = jax.nn.silu(proj[:, :, :, 0]) * proj[:, :, :, 1]
    hidden = jnp.transpose(hidden, (0, 2, 1, 3)).reshape(EXPERTS, most_slots, FE)
    returned = (
        lax.all_to_all(hidden.astype(jnp.bfloat16), EXP, split_axis=0, concat_axis=0, tiled=True)
        .astype(jnp.float32)
        .reshape(EXPERTS * most_slots, FE)
    )
    picked = jnp.take(returned, target, axis=0)
    routed = (picked * route_weight.reshape(-1)[:, None]).astype(jnp.bfloat16)
    return (mixed, routed.reshape(tok_dev, TOPK, FE))


def solution(mesh):
    n_ctx = mesh.shape["ctx"]
    n_exp = mesh.shape["exp"]
    n_zh = 2
    n_xy = n_ctx // n_zh
    side = int(round(math.sqrt(n_xy)))
    n_zl = n_exp // 2
    fine = Mesh(mesh.devices.reshape(n_zh, side, n_xy // side, n_zl, 2), CTX + EXP)
    tok = CTX + EXP
    in_specs = (
        P(tok, None),
        P(CTX, EXP),
        P(CTX, None),
        P(CTX, None),
        P(),
        P(EXP, None),
        P(),
        P(EXP, None, CTX),
        P(EXP, None, CTX),
        P(tok, None),
        P(tok, None),
    )
    out_specs = (P(tok, None), P(tok, None, None))

    def body(*args):
        return shards(*args, n_ctx=n_ctx, n_xy=n_xy, n_zh=n_zh)

    return jax.shard_map(body, mesh=fine, in_specs=in_specs, out_specs=out_specs, check_vma=False)
```

```python
import math

import jax
import jax.numpy as jnp
import numpy as np
from jax import lax
from jax.sharding import Mesh
from jax.sharding import PartitionSpec as P

D = 4096
HQ = 32
KVH = 2
HD = 128
FE = 768
EXPERTS = 16
TOPK = 8
CH = 64

CTX = ("zh", "x", "y")
EXP = ("zl", "c")


def stored_positions(span_pos, rows):
    span = rows // CH
    table = span[:, None] == jnp.arange(span_pos.shape[0], dtype=jnp.int32)[None, :]
    base = jnp.sum(jnp.where(table, span_pos[None, :], 0), axis=1)
    return base * CH + rows % CH


def doubling_bits(n):
    bits = []
    b = n // 2
    while b >= 1:
        bits.append(b)
        b //= 2
    return bits


def gather_by_doubling(piece, n):
    idx = lax.axis_index(CTX)
    cur = piece
    order = [0]
    for bit in doubling_bits(n):
        other = lax.ppermute(cur, CTX, [(i, i ^ bit) for i in range(n)])
        low = (idx & bit) == 0
        cur = jnp.where(low, jnp.concatenate([cur, other]), jnp.concatenate([other, cur]))
        order = order + [o + bit for o in order]
    return cur, order


def shards(
    residual,
    queries,
    keys,
    values,
    span_pos,
    out_proj,
    norm_gain,
    expert_gate,
    expert_up,
    expert_ids,
    route_weight,
    n_ctx,
    n_xy,
    n_zh,
):
    tok_rows = queries.shape[0]
    per_device = queries.shape[1] // HD
    group = HQ // KVH
    ctx_index = lax.axis_index(CTX)
    exp_index = lax.axis_index(EXP)
    n_exp = EXPERTS

    fe_dev = expert_gate.shape[2]
    w_local = jnp.concatenate([expert_gate[0].T, expert_up[0].T], axis=0)
    zh_index = lax.axis_index("zh")
    core_index = lax.axis_index("c")

    kv_head = exp_index * per_device // group
    own_keys = lax.dynamic_slice_in_dim(keys, kv_head * HD, HD, 1)
    own_values = lax.dynamic_slice_in_dim(values, kv_head * HD, HD, 1)
    kv_local = jnp.where(core_index == 0, own_keys, own_values)

    bits = doubling_bits(n_ctx)
    first = bits[0]
    n_w = w_local.size
    joint = jnp.concatenate([w_local.reshape(-1), kv_local.reshape(-1)])
    joint = lax.ppermute(joint, CTX, [(i, i ^ first) for i in range(n_ctx)])
    w_other = joint[:n_w].reshape(w_local.shape)
    kv_other = joint[n_w:].reshape(kv_local.shape)
    w_pair = jnp.where(
        zh_index == 0,
        jnp.concatenate([w_local, w_other]),
        jnp.concatenate([w_other, w_local]),
    )
    w_all = lax.all_gather(w_pair, ("x", "y"), axis=0, tiled=True)

    low = (ctx_index & first) == 0
    cur = jnp.where(
        low, jnp.concatenate([kv_local, kv_other]), jnp.concatenate([kv_other, kv_local])
    )
    order = [0, first]
    for bit in bits[1:]:
        other = lax.ppermute(cur, CTX, [(i, i ^ bit) for i in range(n_ctx)])
        low = (ctx_index & bit) == 0
        cur = jnp.where(low, jnp.concatenate([cur, other]), jnp.concatenate([other, cur]))
        order = order + [o + bit for o in order]
    partner = lax.ppermute(cur, "c", [(0, 1), (1, 0)])
    key_piece = jnp.where(core_index == 0, cur, partner)
    value_piece = jnp.where(core_index == 0, partner, cur)
    length = key_piece.shape[0]
    block_ctx = jnp.asarray(np.array(order, np.int32))
    key_rows_all = (
        jnp.repeat(block_ctx, tok_rows) * tok_rows
        + jnp.tile(jnp.arange(tok_rows, dtype=jnp.int32), n_ctx)
    )

    query_pos = stored_positions(
        span_pos, ctx_index * tok_rows + jnp.arange(tok_rows, dtype=jnp.int32)
    )
    query_heads = queries.reshape(tok_rows, per_device, HD)
    scale = 1.0 / math.sqrt(HD)
    carry = (
        jnp.full((per_device, tok_rows), -1e30, jnp.float32),
        jnp.zeros((per_device, tok_rows), jnp.float32),
        jnp.zeros((per_device, tok_rows, HD), jnp.float32),
    )
    block = min(length, 1024)
    for begin in range(0, length, block):
        stop = min(begin + block, length)
        attend_key_piece = key_piece[begin:stop]
        attend_value_piece = value_piece[begin:stop]
        attend_running, attend_total, attend_accum = carry
        key_pos = stored_positions(span_pos, key_rows_all[begin:stop])
        scores = (
            jnp.einsum(
                "tqd,nd->qtn", query_heads, attend_key_piece, preferred_element_type=jnp.float32
            )
            * scale
        )
        visible = key_pos[None, None, :] <= query_pos[None, :, None]
        block_top = jnp.max(jnp.where(visible, scores, -1e30), axis=2)
        new_top = jnp.maximum(attend_running, block_top)
        factor = jnp.exp(attend_running - new_top)
        probs = jnp.where(visible, jnp.exp(scores - new_top[:, :, None]), 0.0)
        attend_total = attend_total * factor + jnp.sum(probs, axis=2)
        summed = jnp.einsum(
            "qtn,nd->qtd",
            probs.astype(jnp.bfloat16),
            attend_value_piece,
            preferred_element_type=jnp.float32,
        )
        attend_accum = attend_accum * factor[:, :, None] + summed
        carry = (new_top, attend_total, attend_accum)
    running, total, accum = carry
    attn = (accum / total[:, :, None]).astype(jnp.bfloat16)
    attn = jnp.transpose(attn, (1, 0, 2)).reshape(tok_rows, per_device * HD)
    tok_dev = residual.shape[0]

    share = jnp.dot(attn, out_proj, preferred_element_type=jnp.float32).astype(jnp.bfloat16)
    by_core = jnp.transpose(share.reshape(n_exp // 2, 2, tok_dev, D), (1, 0, 2, 3))
    keep = jnp.where(core_index == 0, by_core[0], by_core[1])
    give = jnp.where(core_index == 0, by_core[1], by_core[0])
    got = lax.ppermute(give, "c", [(0, 1), (1, 0)])
    pair_sum = (keep.astype(jnp.float32) + got.astype(jnp.float32)).astype(jnp.bfloat16)
    shares = lax.all_to_all(pair_sum, "zl", split_axis=0, concat_axis=0, tiled=True)
    head_total = jnp.sum(shares.astype(jnp.float32), axis=0)
    mixed = (residual.astype(jnp.float32) + head_total).astype(jnp.bfloat16)
    mixed_f = mixed.astype(jnp.float32)
    square = jnp.mean(mixed_f * mixed_f, axis=1, keepdims=True)
    normed = (mixed_f * lax.rsqrt(square + 1e-06) * norm_gain[None, :]).astype(jnp.bfloat16)

    most_slots = 3 * tok_dev // 4
    ids_flat = expert_ids.reshape(-1)
    onehot = (ids_flat[:, None] == jnp.arange(EXPERTS, dtype=jnp.int32)[None, :]).astype(jnp.int32)
    earlier = jnp.cumsum(onehot, axis=0) - onehot
    slot = jnp.sum(earlier * onehot, axis=1)
    target = ids_flat * most_slots + slot
    placing = (
        target[:, None] == jnp.arange(EXPERTS * most_slots, dtype=jnp.int32)[None, :]
    ).astype(jnp.bfloat16)
    placing = jnp.sum(placing.reshape(tok_dev, TOPK, EXPERTS * most_slots), axis=1)
    outgoing = jnp.einsum("ts,td->sd", placing, normed, preferred_element_type=jnp.float32).astype(
        jnp.bfloat16
    )
    outgoing = outgoing.reshape(EXPERTS, most_slots, D)
    received = lax.all_to_all(outgoing, EXP, split_axis=0, concat_axis=0, tiled=True)
    received = received.reshape(EXPERTS * most_slots, D)

    proj = jnp.einsum("sd,fd->sf", received, w_all, preferred_element_type=jnp.float32)
    proj = proj.reshape(EXPERTS * most_slots, n_xy, n_zh, 2, fe_dev)
    hidden = jax.nn.silu(proj[:, :, :, 0]) * proj[:, :, :, 1]
    hidden = jnp.transpose(hidden, (0, 2, 1, 3)).reshape(EXPERTS, most_slots, FE)
    returned = (
        lax.all_to_all(hidden.astype(jnp.bfloat16), EXP, split_axis=0, concat_axis=0, tiled=True)
        .astype(jnp.float32)
        .reshape(EXPERTS * most_slots, FE)
    )
    picked = jnp.take(returned, target, axis=0)
    routed = (picked * route_weight.reshape(-1)[:, None]).astype(jnp.bfloat16)
    return (mixed, routed.reshape(tok_dev, TOPK, FE))


def solution(mesh):
    n_ctx = mesh.shape["ctx"]
    n_exp = mesh.shape["exp"]
    n_zh = 2
    n_xy = n_ctx // n_zh
    side = int(round(math.sqrt(n_xy)))
    n_zl = n_exp // 2
    fine = Mesh(mesh.devices.reshape(n_zh, side, n_xy // side, n_zl, 2), CTX + EXP)
    tok = CTX + EXP
    in_specs = (
        P(tok, None),
        P(CTX, EXP),
        P(CTX, None),
        P(CTX, None),
        P(),
        P(EXP, None),
        P(),
        P(EXP, None, CTX),
        P(EXP, None, CTX),
        P(tok, None),
        P(tok, None),
    )
    out_specs = (P(tok, None), P(tok, None, None))

    def body(*args):
        return shards(*args, n_ctx=n_ctx, n_xy=n_xy, n_zh=n_zh)

    return jax.shard_map(body, mesh=fine, in_specs=in_specs, out_specs=out_specs, check_vma=False)
```

```python
import math

import jax
import jax.numpy as jnp
import numpy as np
from jax import lax
from jax.sharding import Mesh
from jax.sharding import PartitionSpec as P

D = 4096
HQ = 32
KVH = 2
HD = 128
FE = 768
EXPERTS = 16
TOPK = 8
CH = 64

CTX = ("zh", "x", "y")
EXP = ("zl", "c")


def stored_positions(span_pos, rows):
    span = rows // CH
    table = span[:, None] == jnp.arange(span_pos.shape[0], dtype=jnp.int32)[None, :]
    base = jnp.sum(jnp.where(table, span_pos[None, :], 0), axis=1)
    return base * CH + rows % CH


def doubling_bits(n):
    bits = []
    b = n // 2
    while b >= 1:
        bits.append(b)
        b //= 2
    return bits


def gather_by_doubling(piece, n):
    idx = lax.axis_index(CTX)
    cur = piece
    order = [0]
    for bit in doubling_bits(n):
        other = lax.ppermute(cur, CTX, [(i, i ^ bit) for i in range(n)])
        low = (idx & bit) == 0
        cur = jnp.where(low, jnp.concatenate([cur, other]), jnp.concatenate([other, cur]))
        order = order + [o + bit for o in order]
    return cur, order


def shards(
    residual,
    queries,
    keys,
    values,
    span_pos,
    out_proj,
    norm_gain,
    expert_gate,
    expert_up,
    expert_ids,
    route_weight,
    n_ctx,
    n_xy,
    n_zh,
):
    tok_rows = queries.shape[0]
    per_device = queries.shape[1] // HD
    group = HQ // KVH
    ctx_index = lax.axis_index(CTX)
    exp_index = lax.axis_index(EXP)
    n_exp = EXPERTS

    fe_dev = expert_gate.shape[2]
    w_local = jnp.concatenate([expert_gate[0].T, expert_up[0].T], axis=0)
    zh_index = lax.axis_index("zh")
    core_index = lax.axis_index("c")

    kv_head = exp_index * per_device // group
    own_keys = lax.dynamic_slice_in_dim(keys, kv_head * HD, HD, 1)
    own_values = lax.dynamic_slice_in_dim(values, kv_head * HD, HD, 1)
    kv_local = jnp.where(core_index == 0, own_keys, own_values)

    bits = doubling_bits(n_ctx)
    first = bits[0]
    n_w = w_local.size
    joint = jnp.concatenate([w_local.reshape(-1), kv_local.reshape(-1)])
    joint = lax.ppermute(joint, CTX, [(i, i ^ first) for i in range(n_ctx)])
    w_other = joint[:n_w].reshape(w_local.shape)
    kv_other = joint[n_w:].reshape(kv_local.shape)
    w_pair = jnp.where(
        zh_index == 0,
        jnp.concatenate([w_local, w_other]),
        jnp.concatenate([w_other, w_local]),
    )

    low = (ctx_index & first) == 0
    cur = jnp.where(
        low, jnp.concatenate([kv_local, kv_other]), jnp.concatenate([kv_other, kv_local])
    )
    order = [0, first]
    for bit in bits[1:]:
        other = lax.ppermute(cur, CTX, [(i, i ^ bit) for i in range(n_ctx)])
        low = (ctx_index & bit) == 0
        cur = jnp.where(low, jnp.concatenate([cur, other]), jnp.concatenate([other, cur]))
        order = order + [o + bit for o in order]
    partner = lax.ppermute(cur, "c", [(0, 1), (1, 0)])
    key_piece = jnp.where(core_index == 0, cur, partner)
    value_piece = jnp.where(core_index == 0, partner, cur)
    w_pair, key_piece, value_piece = lax.optimization_barrier((w_pair, key_piece, value_piece))
    w_all = lax.all_gather(w_pair, ("x", "y"), axis=0, tiled=True)
    length = key_piece.shape[0]
    block_ctx = jnp.asarray(np.array(order, np.int32))
    key_rows_all = (
        jnp.repeat(block_ctx, tok_rows) * tok_rows
        + jnp.tile(jnp.arange(tok_rows, dtype=jnp.int32), n_ctx)
    )

    query_pos = stored_positions(
        span_pos, ctx_index * tok_rows + jnp.arange(tok_rows, dtype=jnp.int32)
    )
    query_heads = queries.reshape(tok_rows, per_device, HD)
    scale = 1.0 / math.sqrt(HD)
    carry = (
        jnp.full((per_device, tok_rows), -1e30, jnp.float32),
        jnp.zeros((per_device, tok_rows), jnp.float32),
        jnp.zeros((per_device, tok_rows, HD), jnp.float32),
    )
    block = min(length, 1024)
    for begin in range(0, length, block):
        stop = min(begin + block, length)
        attend_key_piece = key_piece[begin:stop]
        attend_value_piece = value_piece[begin:stop]
        attend_running, attend_total, attend_accum = carry
        key_pos = stored_positions(span_pos, key_rows_all[begin:stop])
        scores = (
            jnp.einsum(
                "tqd,nd->qtn", query_heads, attend_key_piece, preferred_element_type=jnp.float32
            )
            * scale
        )
        visible = key_pos[None, None, :] <= query_pos[None, :, None]
        block_top = jnp.max(jnp.where(visible, scores, -1e30), axis=2)
        new_top = jnp.maximum(attend_running, block_top)
        factor = jnp.exp(attend_running - new_top)
        probs = jnp.where(visible, jnp.exp(scores - new_top[:, :, None]), 0.0)
        attend_total = attend_total * factor + jnp.sum(probs, axis=2)
        summed = jnp.einsum(
            "qtn,nd->qtd",
            probs.astype(jnp.bfloat16),
            attend_value_piece,
            preferred_element_type=jnp.float32,
        )
        attend_accum = attend_accum * factor[:, :, None] + summed
        carry = (new_top, attend_total, attend_accum)
    running, total, accum = carry
    attn = (accum / total[:, :, None]).astype(jnp.bfloat16)
    attn = jnp.transpose(attn, (1, 0, 2)).reshape(tok_rows, per_device * HD)
    tok_dev = residual.shape[0]

    share = jnp.dot(attn, out_proj, preferred_element_type=jnp.float32).astype(jnp.bfloat16)
    by_core = jnp.transpose(share.reshape(n_exp // 2, 2, tok_dev, D), (1, 0, 2, 3))
    keep = jnp.where(core_index == 0, by_core[0], by_core[1])
    give = jnp.where(core_index == 0, by_core[1], by_core[0])
    got = lax.ppermute(give, "c", [(0, 1), (1, 0)])
    pair_sum = (keep.astype(jnp.float32) + got.astype(jnp.float32)).astype(jnp.bfloat16)
    shares = lax.all_to_all(pair_sum, "zl", split_axis=0, concat_axis=0, tiled=True)
    head_total = jnp.sum(shares.astype(jnp.float32), axis=0)
    mixed = (residual.astype(jnp.float32) + head_total).astype(jnp.bfloat16)
    mixed_f = mixed.astype(jnp.float32)
    square = jnp.mean(mixed_f * mixed_f, axis=1, keepdims=True)
    normed = (mixed_f * lax.rsqrt(square + 1e-06) * norm_gain[None, :]).astype(jnp.bfloat16)

    most_slots = 3 * tok_dev // 4
    ids_flat = expert_ids.reshape(-1)
    onehot = (ids_flat[:, None] == jnp.arange(EXPERTS, dtype=jnp.int32)[None, :]).astype(jnp.int32)
    earlier = jnp.cumsum(onehot, axis=0) - onehot
    slot = jnp.sum(earlier * onehot, axis=1)
    target = ids_flat * most_slots + slot
    placing = (
        target[:, None] == jnp.arange(EXPERTS * most_slots, dtype=jnp.int32)[None, :]
    ).astype(jnp.bfloat16)
    placing = jnp.sum(placing.reshape(tok_dev, TOPK, EXPERTS * most_slots), axis=1)
    outgoing = jnp.einsum("ts,td->sd", placing, normed, preferred_element_type=jnp.float32).astype(
        jnp.bfloat16
    )
    outgoing = outgoing.reshape(EXPERTS, most_slots, D)
    received = lax.all_to_all(outgoing, EXP, split_axis=0, concat_axis=0, tiled=True)
    received = received.reshape(EXPERTS * most_slots, D)

    proj = jnp.einsum("sd,fd->sf", received, w_all, preferred_element_type=jnp.float32)
    proj = proj.reshape(EXPERTS * most_slots, n_xy, n_zh, 2, fe_dev)
    hidden = jax.nn.silu(proj[:, :, :, 0]) * proj[:, :, :, 1]
    hidden = jnp.transpose(hidden, (0, 2, 1, 3)).reshape(EXPERTS, most_slots, FE)
    returned = (
        lax.all_to_all(hidden.astype(jnp.bfloat16), EXP, split_axis=0, concat_axis=0, tiled=True)
        .astype(jnp.float32)
        .reshape(EXPERTS * most_slots, FE)
    )
    picked = jnp.take(returned, target, axis=0)
    routed = (picked * route_weight.reshape(-1)[:, None]).astype(jnp.bfloat16)
    return (mixed, routed.reshape(tok_dev, TOPK, FE))


def solution(mesh):
    n_ctx = mesh.shape["ctx"]
    n_exp = mesh.shape["exp"]
    n_zh = 2
    n_xy = n_ctx // n_zh
    side = int(round(math.sqrt(n_xy)))
    n_zl = n_exp // 2
    fine = Mesh(mesh.devices.reshape(n_zh, side, n_xy // side, n_zl, 2), CTX + EXP)
    tok = CTX + EXP
    in_specs = (
        P(tok, None),
        P(CTX, EXP),
        P(CTX, None),
        P(CTX, None),
        P(),
        P(EXP, None),
        P(),
        P(EXP, None, CTX),
        P(EXP, None, CTX),
        P(tok, None),
        P(tok, None),
    )
    out_specs = (P(tok, None), P(tok, None, None))

    def body(*args):
        return shards(*args, n_ctx=n_ctx, n_xy=n_xy, n_zh=n_zh)

    return jax.shard_map(body, mesh=fine, in_specs=in_specs, out_specs=out_specs, check_vma=False)
```

```python
import math

import jax
import jax.numpy as jnp
import numpy as np
from jax import lax
from jax.sharding import Mesh
from jax.sharding import PartitionSpec as P

D = 4096
HQ = 32
KVH = 2
HD = 128
FE = 768
EXPERTS = 16
TOPK = 8
CH = 64

CTX = ("zh", "x", "y")
EXP = ("zl", "c")


def stored_positions(span_pos, rows):
    span = rows // CH
    table = span[:, None] == jnp.arange(span_pos.shape[0], dtype=jnp.int32)[None, :]
    base = jnp.sum(jnp.where(table, span_pos[None, :], 0), axis=1)
    return base * CH + rows % CH


def doubling_bits(n):
    bits = []
    b = n // 2
    while b >= 1:
        bits.append(b)
        b //= 2
    return bits


def gather_by_doubling(piece, n):
    idx = lax.axis_index(CTX)
    cur = piece
    order = [0]
    for bit in doubling_bits(n):
        other = lax.ppermute(cur, CTX, [(i, i ^ bit) for i in range(n)])
        low = (idx & bit) == 0
        cur = jnp.where(low, jnp.concatenate([cur, other]), jnp.concatenate([other, cur]))
        order = order + [o + bit for o in order]
    return cur, order


def shards(
    residual,
    queries,
    keys,
    values,
    span_pos,
    out_proj,
    norm_gain,
    expert_gate,
    expert_up,
    expert_ids,
    route_weight,
    n_ctx,
    n_xy,
    n_zh,
):
    tok_rows = queries.shape[0]
    per_device = queries.shape[1] // HD
    group = HQ // KVH
    ctx_index = lax.axis_index(CTX)
    exp_index = lax.axis_index(EXP)
    n_exp = EXPERTS

    fe_dev = expert_gate.shape[2]
    w_local = jnp.concatenate([expert_gate[0].T, expert_up[0].T], axis=0)
    zh_index = lax.axis_index("zh")
    core_index = lax.axis_index("c")

    kv_head = exp_index * per_device // group
    own_keys = lax.dynamic_slice_in_dim(keys, kv_head * HD, HD, 1)
    own_values = lax.dynamic_slice_in_dim(values, kv_head * HD, HD, 1)
    kv_local = jnp.where(core_index == 0, own_keys, own_values)

    bits = doubling_bits(n_ctx)
    first = bits[0]
    n_w = w_local.size
    joint = jnp.concatenate([w_local.reshape(-1), kv_local.reshape(-1)])
    joint = lax.ppermute(joint, CTX, [(i, i ^ first) for i in range(n_ctx)])
    w_other = joint[:n_w].reshape(w_local.shape)
    kv_other = joint[n_w:].reshape(kv_local.shape)
    w_pair = jnp.where(
        zh_index == 0,
        jnp.concatenate([w_local, w_other]),
        jnp.concatenate([w_other, w_local]),
    )
    w_all = lax.all_gather(w_pair, ("x", "y"), axis=0, tiled=True)

    low = (ctx_index & first) == 0
    cur = jnp.where(
        low, jnp.concatenate([kv_local, kv_other]), jnp.concatenate([kv_other, kv_local])
    )
    order = [0, first]
    for bit in bits[1:]:
        other = lax.ppermute(cur, CTX, [(i, i ^ bit) for i in range(n_ctx)])
        low = (ctx_index & bit) == 0
        cur = jnp.where(low, jnp.concatenate([cur, other]), jnp.concatenate([other, cur]))
        order = order + [o + bit for o in order]
    partner = lax.ppermute(cur, "c", [(0, 1), (1, 0)])
    key_piece = jnp.where(core_index == 0, cur, partner)
    value_piece = jnp.where(core_index == 0, partner, cur)
    length = key_piece.shape[0]
    block_ctx = jnp.asarray(np.array(order, np.int32))
    key_rows_all = (
        jnp.repeat(block_ctx, tok_rows) * tok_rows
        + jnp.tile(jnp.arange(tok_rows, dtype=jnp.int32), n_ctx)
    )

    query_pos = stored_positions(
        span_pos, ctx_index * tok_rows + jnp.arange(tok_rows, dtype=jnp.int32)
    )
    query_heads = queries.reshape(tok_rows, per_device, HD)
    scale = 1.0 / math.sqrt(HD)
    carry = (
        jnp.full((per_device, tok_rows), -1e30, jnp.float32),
        jnp.zeros((per_device, tok_rows), jnp.float32),
        jnp.zeros((per_device, tok_rows, HD), jnp.float32),
    )
    block = min(length, 1024)
    for begin in range(0, length, block):
        stop = min(begin + block, length)
        attend_key_piece = key_piece[begin:stop]
        attend_value_piece = value_piece[begin:stop]
        attend_running, attend_total, attend_accum = carry
        key_pos = stored_positions(span_pos, key_rows_all[begin:stop])
        scores = (
            jnp.einsum(
                "tqd,nd->qtn", query_heads, attend_key_piece, preferred_element_type=jnp.float32
            )
            * scale
        )
        visible = key_pos[None, None, :] <= query_pos[None, :, None]
        block_top = jnp.max(jnp.where(visible, scores, -1e30), axis=2)
        new_top = jnp.maximum(attend_running, block_top)
        factor = jnp.exp(attend_running - new_top)
        probs = jnp.where(visible, jnp.exp(scores - new_top[:, :, None]), 0.0)
        attend_total = attend_total * factor + jnp.sum(probs, axis=2)
        summed = jnp.einsum(
            "qtn,nd->qtd",
            probs.astype(jnp.bfloat16),
            attend_value_piece,
            preferred_element_type=jnp.float32,
        )
        attend_accum = attend_accum * factor[:, :, None] + summed
        carry = (new_top, attend_total, attend_accum)
    running, total, accum = carry
    attn = (accum / total[:, :, None]).astype(jnp.bfloat16)
    attn = jnp.transpose(attn, (1, 0, 2)).reshape(tok_rows, per_device * HD)
    tok_dev = residual.shape[0]

    share = jnp.dot(attn, out_proj, preferred_element_type=jnp.float32).astype(jnp.bfloat16)
    zl_index = lax.axis_index("zl")
    n_zl = n_exp // 2
    by_core = jnp.transpose(share.reshape(n_zl, 2, tok_dev, D), (1, 0, 2, 3))
    keep = jnp.where(core_index == 0, by_core[0], by_core[1])
    give = jnp.where(core_index == 0, by_core[1], by_core[0])
    got = lax.ppermute(give, "c", [(0, 1), (1, 0)])
    part = keep.astype(jnp.float32) + got.astype(jnp.float32)
    zl_bits = doubling_bits(n_zl)[::-1]
    part = part.reshape((2,) * len(zl_bits) + (tok_dev, D))
    for step, bit in enumerate(zl_bits):
        axis = len(zl_bits) - 1 - step
        mine = (zl_index & bit) == 0
        lo = lax.index_in_dim(part, 0, axis, keepdims=False)
        hi = lax.index_in_dim(part, 1, axis, keepdims=False)
        stay = jnp.where(mine, lo, hi)
        send = jnp.where(mine, hi, lo)
        part = stay + lax.ppermute(send, "zl", [(i, i ^ bit) for i in range(n_zl)])
    head_total = part
    mixed = (residual.astype(jnp.float32) + head_total).astype(jnp.bfloat16)
    mixed_f = mixed.astype(jnp.float32)
    square = jnp.mean(mixed_f * mixed_f, axis=1, keepdims=True)
    normed = (mixed_f * lax.rsqrt(square + 1e-06) * norm_gain[None, :]).astype(jnp.bfloat16)

    ids_pad = jnp.zeros((tok_dev, 128), jnp.bfloat16).at[:, :TOPK].set(
        expert_ids.astype(jnp.bfloat16)
    )
    cur = jnp.concatenate([normed, ids_pad], axis=1)
    order = [0]
    for bit in doubling_bits(n_zl):
        other = lax.ppermute(cur, "zl", [(i, i ^ bit) for i in range(n_zl)])
        low = (zl_index & bit) == 0
        cur = jnp.where(low, jnp.concatenate([cur, other]), jnp.concatenate([other, cur]))
        order = order + [o + bit for o in order]
    partner = lax.ppermute(cur, "c", [(0, 1), (1, 0)])
    both = jnp.where(
        core_index == 0, jnp.concatenate([cur, partner]), jnp.concatenate([partner, cur])
    )
    blocks = []
    for src in range(n_exp):
        q = (src % 2) * n_zl + order.index(src // 2)
        blocks.append(both[q * tok_dev : (q + 1) * tok_dev])
    gathered = jnp.concatenate(blocks)
    normed_all = gathered[:, :D]
    ids_all = gathered[:, D : D + TOPK].astype(jnp.int32)

    most_slots = 3 * tok_dev // 4
    chosen = jnp.any(ids_all == exp_index, axis=1).astype(jnp.int32).reshape(n_exp, tok_dev)
    rank = jnp.cumsum(chosen, axis=1) - chosen
    dest = jnp.where(
        chosen == 1, jnp.arange(n_exp, dtype=jnp.int32)[:, None] * most_slots + rank, -1
    ).reshape(-1)
    placing = (
        jnp.arange(n_exp * most_slots, dtype=jnp.int32)[:, None] == dest[None, :]
    ).astype(jnp.bfloat16)
    received = jnp.dot(placing, normed_all, preferred_element_type=jnp.float32).astype(
        jnp.bfloat16
    )

    ids_flat = expert_ids.reshape(-1)
    onehot = (ids_flat[:, None] == jnp.arange(EXPERTS, dtype=jnp.int32)[None, :]).astype(jnp.int32)
    earlier = jnp.cumsum(onehot, axis=0) - onehot
    slot = jnp.sum(earlier * onehot, axis=1)
    target = ids_flat * most_slots + slot

    proj = jnp.einsum("sd,fd->sf", received, w_all, preferred_element_type=jnp.float32)
    proj = proj.reshape(EXPERTS * most_slots, n_xy, n_zh, 2, fe_dev)
    hidden = jax.nn.silu(proj[:, :, :, 0]) * proj[:, :, :, 1]
    hidden = jnp.transpose(hidden, (0, 2, 1, 3)).reshape(EXPERTS, most_slots, FE)
    returned = (
        lax.all_to_all(hidden.astype(jnp.bfloat16), EXP, split_axis=0, concat_axis=0, tiled=True)
        .astype(jnp.float32)
        .reshape(EXPERTS * most_slots, FE)
    )
    picked = jnp.take(returned, target, axis=0)
    routed = (picked * route_weight.reshape(-1)[:, None]).astype(jnp.bfloat16)
    return (mixed, routed.reshape(tok_dev, TOPK, FE))


def solution(mesh):
    n_ctx = mesh.shape["ctx"]
    n_exp = mesh.shape["exp"]
    n_zh = 2
    n_xy = n_ctx // n_zh
    side = int(round(math.sqrt(n_xy)))
    n_zl = n_exp // 2
    fine = Mesh(mesh.devices.reshape(n_zh, side, n_xy // side, n_zl, 2), CTX + EXP)
    tok = CTX + EXP
    in_specs = (
        P(tok, None),
        P(CTX, EXP),
        P(CTX, None),
        P(CTX, None),
        P(),
        P(EXP, None),
        P(),
        P(EXP, None, CTX),
        P(EXP, None, CTX),
        P(tok, None),
        P(tok, None),
    )
    out_specs = (P(tok, None), P(tok, None, None))

    def body(*args):
        return shards(*args, n_ctx=n_ctx, n_xy=n_xy, n_zh=n_zh)

    return jax.shard_map(body, mesh=fine, in_specs=in_specs, out_specs=out_specs, check_vma=False)
```

```python
import math

import jax
import jax.numpy as jnp
import numpy as np
from jax import lax
from jax.sharding import Mesh
from jax.sharding import PartitionSpec as P

D = 4096
HQ = 32
KVH = 2
HD = 128
FE = 768
EXPERTS = 16
TOPK = 8
CH = 64

CTX = ("zh", "x", "y")
EXP = ("zl", "c")


def stored_positions(span_pos, rows):
    span = rows // CH
    table = span[:, None] == jnp.arange(span_pos.shape[0], dtype=jnp.int32)[None, :]
    base = jnp.sum(jnp.where(table, span_pos[None, :], 0), axis=1)
    return base * CH + rows % CH


def doubling_bits(n):
    bits = []
    b = n // 2
    while b >= 1:
        bits.append(b)
        b //= 2
    return bits


def gather_by_doubling(piece, n):
    idx = lax.axis_index(CTX)
    cur = piece
    order = [0]
    for bit in doubling_bits(n):
        other = lax.ppermute(cur, CTX, [(i, i ^ bit) for i in range(n)])
        low = (idx & bit) == 0
        cur = jnp.where(low, jnp.concatenate([cur, other]), jnp.concatenate([other, cur]))
        order = order + [o + bit for o in order]
    return cur, order


def shards(
    residual,
    queries,
    keys,
    values,
    span_pos,
    out_proj,
    norm_gain,
    expert_gate,
    expert_up,
    expert_ids,
    route_weight,
    n_ctx,
    n_xy,
    n_zh,
):
    tok_rows = queries.shape[0]
    per_device = queries.shape[1] // HD
    group = HQ // KVH
    ctx_index = lax.axis_index(CTX)
    exp_index = lax.axis_index(EXP)
    n_exp = EXPERTS

    fe_dev = expert_gate.shape[2]
    w_local = jnp.concatenate([expert_gate[0].T, expert_up[0].T], axis=0)
    zh_index = lax.axis_index("zh")
    core_index = lax.axis_index("c")

    kv_head = exp_index * per_device // group
    own_keys = lax.dynamic_slice_in_dim(keys, kv_head * HD, HD, 1)
    own_values = lax.dynamic_slice_in_dim(values, kv_head * HD, HD, 1)
    kv_local = jnp.where(core_index == 0, own_keys, own_values)

    bits = doubling_bits(n_ctx)
    first = bits[0]
    n_w = w_local.size
    joint = jnp.concatenate([w_local.reshape(-1), kv_local.reshape(-1)])
    joint = lax.ppermute(joint, CTX, [(i, i ^ first) for i in range(n_ctx)])
    w_other = joint[:n_w].reshape(w_local.shape)
    kv_other = joint[n_w:].reshape(kv_local.shape)
    w_pair = jnp.where(
        zh_index == 0,
        jnp.concatenate([w_local, w_other]),
        jnp.concatenate([w_other, w_local]),
    )
    w_all = lax.all_gather(w_pair, ("x", "y"), axis=0, tiled=True)

    low = (ctx_index & first) == 0
    cur = jnp.where(
        low, jnp.concatenate([kv_local, kv_other]), jnp.concatenate([kv_other, kv_local])
    )
    order = [0, first]
    for bit in bits[1:]:
        other = lax.ppermute(cur, CTX, [(i, i ^ bit) for i in range(n_ctx)])
        low = (ctx_index & bit) == 0
        cur = jnp.where(low, jnp.concatenate([cur, other]), jnp.concatenate([other, cur]))
        order = order + [o + bit for o in order]
    partner = lax.ppermute(cur, "c", [(0, 1), (1, 0)])
    key_piece = jnp.where(core_index == 0, cur, partner)
    value_piece = jnp.where(core_index == 0, partner, cur)
    length = key_piece.shape[0]
    block_ctx = jnp.asarray(np.array(order, np.int32))
    key_rows_all = (
        jnp.repeat(block_ctx, tok_rows) * tok_rows
        + jnp.tile(jnp.arange(tok_rows, dtype=jnp.int32), n_ctx)
    )

    query_pos = stored_positions(
        span_pos, ctx_index * tok_rows + jnp.arange(tok_rows, dtype=jnp.int32)
    )
    query_heads = queries.reshape(tok_rows, per_device, HD)
    scale = 1.0 / math.sqrt(HD)
    carry = (
        jnp.full((per_device, tok_rows), -1e30, jnp.float32),
        jnp.zeros((per_device, tok_rows), jnp.float32),
        jnp.zeros((per_device, tok_rows, HD), jnp.float32),
    )
    block = min(length, 1024)
    for begin in range(0, length, block):
        stop = min(begin + block, length)
        attend_key_piece = key_piece[begin:stop]
        attend_value_piece = value_piece[begin:stop]
        attend_running, attend_total, attend_accum = carry
        key_pos = stored_positions(span_pos, key_rows_all[begin:stop])
        scores = (
            jnp.einsum(
                "tqd,nd->qtn", query_heads, attend_key_piece, preferred_element_type=jnp.float32
            )
            * scale
        )
        visible = key_pos[None, None, :] <= query_pos[None, :, None]
        block_top = jnp.max(jnp.where(visible, scores, -1e30), axis=2)
        new_top = jnp.maximum(attend_running, block_top)
        factor = jnp.exp(attend_running - new_top)
        probs = jnp.where(visible, jnp.exp(scores - new_top[:, :, None]), 0.0)
        attend_total = attend_total * factor + jnp.sum(probs, axis=2)
        summed = jnp.einsum(
            "qtn,nd->qtd",
            probs.astype(jnp.bfloat16),
            attend_value_piece,
            preferred_element_type=jnp.float32,
        )
        attend_accum = attend_accum * factor[:, :, None] + summed
        carry = (new_top, attend_total, attend_accum)
    running, total, accum = carry
    attn = (accum / total[:, :, None]).astype(jnp.bfloat16)
    attn = jnp.transpose(attn, (1, 0, 2)).reshape(tok_rows, per_device * HD)
    tok_dev = residual.shape[0]

    share = jnp.dot(attn, out_proj, preferred_element_type=jnp.float32).astype(jnp.bfloat16)
    zl_index = lax.axis_index("zl")
    n_zl = n_exp // 2
    by_core = jnp.transpose(share.reshape(n_zl, 2, tok_dev, D), (1, 0, 2, 3))
    keep = jnp.where(core_index == 0, by_core[0], by_core[1])
    give = jnp.where(core_index == 0, by_core[1], by_core[0])
    got = lax.ppermute(give, "c", [(0, 1), (1, 0)])
    part = keep.astype(jnp.float32) + got.astype(jnp.float32)
    pair_sum = part.astype(jnp.bfloat16)
    shares = lax.all_to_all(pair_sum, "zl", split_axis=0, concat_axis=0, tiled=True)
    head_total = jnp.sum(shares.astype(jnp.float32), axis=0)
    mixed = (residual.astype(jnp.float32) + head_total).astype(jnp.bfloat16)
    mixed_f = mixed.astype(jnp.float32)
    square = jnp.mean(mixed_f * mixed_f, axis=1, keepdims=True)
    normed = (mixed_f * lax.rsqrt(square + 1e-06) * norm_gain[None, :]).astype(jnp.bfloat16)

    ids_all = lax.all_to_all(
        jnp.broadcast_to(expert_ids[None], (n_exp,) + expert_ids.shape),
        EXP,
        split_axis=0,
        concat_axis=0,
        tiled=True,
    ).reshape(n_exp * tok_dev, TOPK)
    cur = normed
    order = [0]
    for bit in doubling_bits(n_zl):
        other = lax.ppermute(cur, "zl", [(i, i ^ bit) for i in range(n_zl)])
        low = (zl_index & bit) == 0
        cur = jnp.where(low, jnp.concatenate([cur, other]), jnp.concatenate([other, cur]))
        order = order + [o + bit for o in order]
    partner = lax.ppermute(cur, "c", [(0, 1), (1, 0)])
    both = jnp.where(
        core_index == 0, jnp.concatenate([cur, partner]), jnp.concatenate([partner, cur])
    )
    blocks = []
    for src in range(n_exp):
        q = (src % 2) * n_zl + order.index(src // 2)
        blocks.append(both[q * tok_dev : (q + 1) * tok_dev])
    gathered = jnp.concatenate(blocks)
    normed_all = gathered

    most_slots = 3 * tok_dev // 4
    chosen = jnp.any(ids_all == exp_index, axis=1).astype(jnp.int32).reshape(n_exp, tok_dev)
    rank = jnp.cumsum(chosen, axis=1) - chosen
    dest = jnp.where(
        chosen == 1, jnp.arange(n_exp, dtype=jnp.int32)[:, None] * most_slots + rank, -1
    ).reshape(-1)
    placing = (
        jnp.arange(n_exp * most_slots, dtype=jnp.int32)[:, None] == dest[None, :]
    ).astype(jnp.bfloat16)
    received = jnp.dot(placing, normed_all, preferred_element_type=jnp.float32).astype(
        jnp.bfloat16
    )

    ids_flat = expert_ids.reshape(-1)
    onehot = (ids_flat[:, None] == jnp.arange(EXPERTS, dtype=jnp.int32)[None, :]).astype(jnp.int32)
    earlier = jnp.cumsum(onehot, axis=0) - onehot
    slot = jnp.sum(earlier * onehot, axis=1)
    target = ids_flat * most_slots + slot

    proj = jnp.einsum("sd,fd->sf", received, w_all, preferred_element_type=jnp.float32)
    proj = proj.reshape(EXPERTS * most_slots, n_xy, n_zh, 2, fe_dev)
    hidden = jax.nn.silu(proj[:, :, :, 0]) * proj[:, :, :, 1]
    hidden = jnp.transpose(hidden, (0, 2, 1, 3)).reshape(EXPERTS, most_slots, FE)
    returned = (
        lax.all_to_all(hidden.astype(jnp.bfloat16), EXP, split_axis=0, concat_axis=0, tiled=True)
        .astype(jnp.float32)
        .reshape(EXPERTS * most_slots, FE)
    )
    picked = jnp.take(returned, target, axis=0)
    routed = (picked * route_weight.reshape(-1)[:, None]).astype(jnp.bfloat16)
    return (mixed, routed.reshape(tok_dev, TOPK, FE))


def solution(mesh):
    n_ctx = mesh.shape["ctx"]
    n_exp = mesh.shape["exp"]
    n_zh = 2
    n_xy = n_ctx // n_zh
    side = int(round(math.sqrt(n_xy)))
    n_zl = n_exp // 2
    fine = Mesh(mesh.devices.reshape(n_zh, side, n_xy // side, n_zl, 2), CTX + EXP)
    tok = CTX + EXP
    in_specs = (
        P(tok, None),
        P(CTX, EXP),
        P(CTX, None),
        P(CTX, None),
        P(),
        P(EXP, None),
        P(),
        P(EXP, None, CTX),
        P(EXP, None, CTX),
        P(tok, None),
        P(tok, None),
    )
    out_specs = (P(tok, None), P(tok, None, None))

    def body(*args):
        return shards(*args, n_ctx=n_ctx, n_xy=n_xy, n_zh=n_zh)

    return jax.shard_map(body, mesh=fine, in_specs=in_specs, out_specs=out_specs, check_vma=False)
```

```python
import math

import jax
import jax.numpy as jnp
import numpy as np
from jax import lax
from jax.sharding import Mesh
from jax.sharding import PartitionSpec as P

D = 4096
HQ = 32
KVH = 2
HD = 128
FE = 768
EXPERTS = 16
TOPK = 8
CH = 64

CTX = ("zh", "x", "y")
EXP = ("zl", "c")


def stored_positions(span_pos, rows):
    span = rows // CH
    table = span[:, None] == jnp.arange(span_pos.shape[0], dtype=jnp.int32)[None, :]
    base = jnp.sum(jnp.where(table, span_pos[None, :], 0), axis=1)
    return base * CH + rows % CH


def doubling_bits(n):
    bits = []
    b = n // 2
    while b >= 1:
        bits.append(b)
        b //= 2
    return bits


def gather_by_doubling(piece, n):
    idx = lax.axis_index(CTX)
    cur = piece
    order = [0]
    for bit in doubling_bits(n):
        other = lax.ppermute(cur, CTX, [(i, i ^ bit) for i in range(n)])
        low = (idx & bit) == 0
        cur = jnp.where(low, jnp.concatenate([cur, other]), jnp.concatenate([other, cur]))
        order = order + [o + bit for o in order]
    return cur, order


def shards(
    residual,
    queries,
    keys,
    values,
    span_pos,
    out_proj,
    norm_gain,
    expert_gate,
    expert_up,
    expert_ids,
    route_weight,
    n_ctx,
    n_xy,
    n_zh,
):
    tok_rows = queries.shape[0]
    per_device = queries.shape[1] // HD
    group = HQ // KVH
    ctx_index = lax.axis_index(CTX)
    exp_index = lax.axis_index(EXP)
    n_exp = EXPERTS

    fe_dev = expert_gate.shape[2]
    w_local = jnp.concatenate([expert_gate[0].T, expert_up[0].T], axis=0)
    zh_index = lax.axis_index("zh")
    core_index = lax.axis_index("c")

    kv_head = exp_index * per_device // group
    own_keys = lax.dynamic_slice_in_dim(keys, kv_head * HD, HD, 1)
    own_values = lax.dynamic_slice_in_dim(values, kv_head * HD, HD, 1)
    kv_local = jnp.where(core_index == 0, own_keys, own_values)

    bits = doubling_bits(n_ctx)
    first = bits[0]
    kv_other = lax.ppermute(kv_local, CTX, [(i, i ^ first) for i in range(n_ctx)])
    w_other = lax.ppermute(w_local, "zh", [(0, 1), (1, 0)])
    w_pair = jnp.where(
        zh_index == 0,
        jnp.concatenate([w_local, w_other]),
        jnp.concatenate([w_other, w_local]),
    )
    w_all = lax.all_gather(w_pair, ("x", "y"), axis=0, tiled=True)

    low = (ctx_index & first) == 0
    cur = jnp.where(
        low, jnp.concatenate([kv_local, kv_other]), jnp.concatenate([kv_other, kv_local])
    )
    order = [0, first]
    for bit in bits[1:]:
        other = lax.ppermute(cur, CTX, [(i, i ^ bit) for i in range(n_ctx)])
        low = (ctx_index & bit) == 0
        cur = jnp.where(low, jnp.concatenate([cur, other]), jnp.concatenate([other, cur]))
        order = order + [o + bit for o in order]
    partner = lax.ppermute(cur, "c", [(0, 1), (1, 0)])
    key_piece = jnp.where(core_index == 0, cur, partner)
    value_piece = jnp.where(core_index == 0, partner, cur)
    length = key_piece.shape[0]
    block_ctx = jnp.asarray(np.array(order, np.int32))
    key_rows_all = (
        jnp.repeat(block_ctx, tok_rows) * tok_rows
        + jnp.tile(jnp.arange(tok_rows, dtype=jnp.int32), n_ctx)
    )

    query_pos = stored_positions(
        span_pos, ctx_index * tok_rows + jnp.arange(tok_rows, dtype=jnp.int32)
    )
    query_heads = queries.reshape(tok_rows, per_device, HD)
    scale = 1.0 / math.sqrt(HD)
    carry = (
        jnp.full((per_device, tok_rows), -1e30, jnp.float32),
        jnp.zeros((per_device, tok_rows), jnp.float32),
        jnp.zeros((per_device, tok_rows, HD), jnp.float32),
    )
    block = min(length, 1024)
    for begin in range(0, length, block):
        stop = min(begin + block, length)
        attend_key_piece = key_piece[begin:stop]
        attend_value_piece = value_piece[begin:stop]
        attend_running, attend_total, attend_accum = carry
        key_pos = stored_positions(span_pos, key_rows_all[begin:stop])
        scores = (
            jnp.einsum(
                "tqd,nd->qtn", query_heads, attend_key_piece, preferred_element_type=jnp.float32
            )
            * scale
        )
        visible = key_pos[None, None, :] <= query_pos[None, :, None]
        block_top = jnp.max(jnp.where(visible, scores, -1e30), axis=2)
        new_top = jnp.maximum(attend_running, block_top)
        factor = jnp.exp(attend_running - new_top)
        probs = jnp.where(visible, jnp.exp(scores - new_top[:, :, None]), 0.0)
        attend_total = attend_total * factor + jnp.sum(probs, axis=2)
        summed = jnp.einsum(
            "qtn,nd->qtd",
            probs.astype(jnp.bfloat16),
            attend_value_piece,
            preferred_element_type=jnp.float32,
        )
        attend_accum = attend_accum * factor[:, :, None] + summed
        carry = (new_top, attend_total, attend_accum)
    running, total, accum = carry
    attn = (accum / total[:, :, None]).astype(jnp.bfloat16)
    attn = jnp.transpose(attn, (1, 0, 2)).reshape(tok_rows, per_device * HD)
    tok_dev = residual.shape[0]

    share = jnp.dot(attn, out_proj, preferred_element_type=jnp.float32).astype(jnp.bfloat16)
    zl_index = lax.axis_index("zl")
    n_zl = n_exp // 2
    by_core = jnp.transpose(share.reshape(n_zl, 2, tok_dev, D), (1, 0, 2, 3))
    keep = jnp.where(core_index == 0, by_core[0], by_core[1])
    give = jnp.where(core_index == 0, by_core[1], by_core[0])
    got = lax.ppermute(give, "c", [(0, 1), (1, 0)])
    part = keep.astype(jnp.float32) + got.astype(jnp.float32)
    pair_sum = part.astype(jnp.bfloat16)
    shares = lax.all_to_all(pair_sum, "zl", split_axis=0, concat_axis=0, tiled=True)
    head_total = jnp.sum(shares.astype(jnp.float32), axis=0)
    mixed = (residual.astype(jnp.float32) + head_total).astype(jnp.bfloat16)
    mixed_f = mixed.astype(jnp.float32)
    square = jnp.mean(mixed_f * mixed_f, axis=1, keepdims=True)
    normed = (mixed_f * lax.rsqrt(square + 1e-06) * norm_gain[None, :]).astype(jnp.bfloat16)

    ids_all = lax.all_to_all(
        jnp.broadcast_to(expert_ids[None], (n_exp,) + expert_ids.shape),
        EXP,
        split_axis=0,
        concat_axis=0,
        tiled=True,
    ).reshape(n_exp * tok_dev, TOPK)
    cur = normed
    order = [0]
    for bit in doubling_bits(n_zl):
        other = lax.ppermute(cur, "zl", [(i, i ^ bit) for i in range(n_zl)])
        low = (zl_index & bit) == 0
        cur = jnp.where(low, jnp.concatenate([cur, other]), jnp.concatenate([other, cur]))
        order = order + [o + bit for o in order]
    partner = lax.ppermute(cur, "c", [(0, 1), (1, 0)])
    both = jnp.where(
        core_index == 0, jnp.concatenate([cur, partner]), jnp.concatenate([partner, cur])
    )
    blocks = []
    for src in range(n_exp):
        q = (src % 2) * n_zl + order.index(src // 2)
        blocks.append(both[q * tok_dev : (q + 1) * tok_dev])
    gathered = jnp.concatenate(blocks)
    normed_all = gathered

    most_slots = 3 * tok_dev // 4
    chosen = jnp.any(ids_all == exp_index, axis=1).astype(jnp.int32).reshape(n_exp, tok_dev)
    rank = jnp.cumsum(chosen, axis=1) - chosen
    dest = jnp.where(
        chosen == 1, jnp.arange(n_exp, dtype=jnp.int32)[:, None] * most_slots + rank, -1
    ).reshape(-1)
    placing = (
        jnp.arange(n_exp * most_slots, dtype=jnp.int32)[:, None] == dest[None, :]
    ).astype(jnp.bfloat16)
    received = jnp.dot(placing, normed_all, preferred_element_type=jnp.float32).astype(
        jnp.bfloat16
    )

    ids_flat = expert_ids.reshape(-1)
    onehot = (ids_flat[:, None] == jnp.arange(EXPERTS, dtype=jnp.int32)[None, :]).astype(jnp.int32)
    earlier = jnp.cumsum(onehot, axis=0) - onehot
    slot = jnp.sum(earlier * onehot, axis=1)
    target = ids_flat * most_slots + slot

    proj = jnp.einsum("sd,fd->sf", received, w_all, preferred_element_type=jnp.float32)
    proj = proj.reshape(EXPERTS * most_slots, n_xy, n_zh, 2, fe_dev)
    hidden = jax.nn.silu(proj[:, :, :, 0]) * proj[:, :, :, 1]
    hidden = jnp.transpose(hidden, (0, 2, 1, 3)).reshape(EXPERTS, most_slots, FE)
    returned = (
        lax.all_to_all(hidden.astype(jnp.bfloat16), EXP, split_axis=0, concat_axis=0, tiled=True)
        .astype(jnp.float32)
        .reshape(EXPERTS * most_slots, FE)
    )
    picked = jnp.take(returned, target, axis=0)
    routed = (picked * route_weight.reshape(-1)[:, None]).astype(jnp.bfloat16)
    return (mixed, routed.reshape(tok_dev, TOPK, FE))


def solution(mesh):
    n_ctx = mesh.shape["ctx"]
    n_exp = mesh.shape["exp"]
    n_zh = 2
    n_xy = n_ctx // n_zh
    side = int(round(math.sqrt(n_xy)))
    n_zl = n_exp // 2
    fine = Mesh(mesh.devices.reshape(n_zh, side, n_xy // side, n_zl, 2), CTX + EXP)
    tok = CTX + EXP
    in_specs = (
        P(tok, None),
        P(CTX, EXP),
        P(CTX, None),
        P(CTX, None),
        P(),
        P(EXP, None),
        P(),
        P(EXP, None, CTX),
        P(EXP, None, CTX),
        P(tok, None),
        P(tok, None),
    )
    out_specs = (P(tok, None), P(tok, None, None))

    def body(*args):
        return shards(*args, n_ctx=n_ctx, n_xy=n_xy, n_zh=n_zh)

    return jax.shard_map(body, mesh=fine, in_specs=in_specs, out_specs=out_specs, check_vma=False)
```

```python
import math

import jax
import jax.numpy as jnp
import numpy as np
from jax import lax
from jax.sharding import Mesh
from jax.sharding import PartitionSpec as P

D = 4096
HQ = 32
KVH = 2
HD = 128
FE = 768
EXPERTS = 16
TOPK = 8
CH = 64

CTX = ("zh", "x", "y")
EXP = ("zl", "c")


def stored_positions(span_pos, rows):
    span = rows // CH
    table = span[:, None] == jnp.arange(span_pos.shape[0], dtype=jnp.int32)[None, :]
    base = jnp.sum(jnp.where(table, span_pos[None, :], 0), axis=1)
    return base * CH + rows % CH


def doubling_bits(n):
    bits = []
    b = n // 2
    while b >= 1:
        bits.append(b)
        b //= 2
    return bits


def gather_by_doubling(piece, n):
    idx = lax.axis_index(CTX)
    cur = piece
    order = [0]
    for bit in doubling_bits(n):
        other = lax.ppermute(cur, CTX, [(i, i ^ bit) for i in range(n)])
        low = (idx & bit) == 0
        cur = jnp.where(low, jnp.concatenate([cur, other]), jnp.concatenate([other, cur]))
        order = order + [o + bit for o in order]
    return cur, order


def shards(
    residual,
    queries,
    keys,
    values,
    span_pos,
    out_proj,
    norm_gain,
    expert_gate,
    expert_up,
    expert_ids,
    route_weight,
    n_ctx,
    n_xy,
    n_zh,
):
    tok_rows = queries.shape[0]
    per_device = queries.shape[1] // HD
    group = HQ // KVH
    ctx_index = lax.axis_index(CTX)
    exp_index = lax.axis_index(EXP)
    n_exp = EXPERTS

    fe_dev = expert_gate.shape[2]
    w_local = jnp.concatenate([expert_gate[0].T, expert_up[0].T], axis=0)
    zh_index = lax.axis_index("zh")
    core_index = lax.axis_index("c")

    kv_head = exp_index * per_device // group
    own_keys = lax.dynamic_slice_in_dim(keys, kv_head * HD, HD, 1)
    own_values = lax.dynamic_slice_in_dim(values, kv_head * HD, HD, 1)
    kv_local = jnp.where(core_index == 0, own_keys, own_values)

    bits = doubling_bits(n_ctx)
    first = bits[0]
    kv_other = lax.ppermute(kv_local, CTX, [(i, i ^ first) for i in range(n_ctx)])
    w_other = lax.ppermute(w_local, "zh", [(0, 1), (1, 0)])
    w_pair = jnp.where(
        zh_index == 0,
        jnp.concatenate([w_local, w_other]),
        jnp.concatenate([w_other, w_local]),
    )
    w_all = lax.all_gather(w_pair, ("x", "y"), axis=0, tiled=True)

    low = (ctx_index & first) == 0
    cur = jnp.where(
        low, jnp.concatenate([kv_local, kv_other]), jnp.concatenate([kv_other, kv_local])
    )
    order = [0, first]
    for step, bit in enumerate(bits[1:]):
        other = lax.ppermute(cur, CTX, [(i, i ^ bit) for i in range(n_ctx)])
        low = (ctx_index & bit) == 0
        cur = jnp.where(low, jnp.concatenate([cur, other]), jnp.concatenate([other, cur]))
        order = order + [o + bit for o in order]
        if step == 0:
            w_pair, cur = lax.optimization_barrier((w_pair, cur))
    partner = lax.ppermute(cur, "c", [(0, 1), (1, 0)])
    key_piece = jnp.where(core_index == 0, cur, partner)
    value_piece = jnp.where(core_index == 0, partner, cur)
    length = key_piece.shape[0]
    block_ctx = jnp.asarray(np.array(order, np.int32))
    key_rows_all = (
        jnp.repeat(block_ctx, tok_rows) * tok_rows
        + jnp.tile(jnp.arange(tok_rows, dtype=jnp.int32), n_ctx)
    )

    query_pos = stored_positions(
        span_pos, ctx_index * tok_rows + jnp.arange(tok_rows, dtype=jnp.int32)
    )
    query_heads = queries.reshape(tok_rows, per_device, HD)
    scale = 1.0 / math.sqrt(HD)
    carry = (
        jnp.full((per_device, tok_rows), -1e30, jnp.float32),
        jnp.zeros((per_device, tok_rows), jnp.float32),
        jnp.zeros((per_device, tok_rows, HD), jnp.float32),
    )
    block = min(length, 1024)
    for begin in range(0, length, block):
        stop = min(begin + block, length)
        attend_key_piece = key_piece[begin:stop]
        attend_value_piece = value_piece[begin:stop]
        attend_running, attend_total, attend_accum = carry
        key_pos = stored_positions(span_pos, key_rows_all[begin:stop])
        scores = (
            jnp.einsum(
                "tqd,nd->qtn", query_heads, attend_key_piece, preferred_element_type=jnp.float32
            )
            * scale
        )
        visible = key_pos[None, None, :] <= query_pos[None, :, None]
        block_top = jnp.max(jnp.where(visible, scores, -1e30), axis=2)
        new_top = jnp.maximum(attend_running, block_top)
        factor = jnp.exp(attend_running - new_top)
        probs = jnp.where(visible, jnp.exp(scores - new_top[:, :, None]), 0.0)
        attend_total = attend_total * factor + jnp.sum(probs, axis=2)
        summed = jnp.einsum(
            "qtn,nd->qtd",
            probs.astype(jnp.bfloat16),
            attend_value_piece,
            preferred_element_type=jnp.float32,
        )
        attend_accum = attend_accum * factor[:, :, None] + summed
        carry = (new_top, attend_total, attend_accum)
    running, total, accum = carry
    attn = (accum / total[:, :, None]).astype(jnp.bfloat16)
    attn = jnp.transpose(attn, (1, 0, 2)).reshape(tok_rows, per_device * HD)
    tok_dev = residual.shape[0]

    share = jnp.dot(attn, out_proj, preferred_element_type=jnp.float32).astype(jnp.bfloat16)
    zl_index = lax.axis_index("zl")
    n_zl = n_exp // 2
    by_core = jnp.transpose(share.reshape(n_zl, 2, tok_dev, D), (1, 0, 2, 3))
    keep = jnp.where(core_index == 0, by_core[0], by_core[1])
    give = jnp.where(core_index == 0, by_core[1], by_core[0])
    got = lax.ppermute(give, "c", [(0, 1), (1, 0)])
    part = keep.astype(jnp.float32) + got.astype(jnp.float32)
    pair_sum = part.astype(jnp.bfloat16)
    shares = lax.all_to_all(pair_sum, "zl", split_axis=0, concat_axis=0, tiled=True)
    head_total = jnp.sum(shares.astype(jnp.float32), axis=0)
    mixed = (residual.astype(jnp.float32) + head_total).astype(jnp.bfloat16)
    mixed_f = mixed.astype(jnp.float32)
    square = jnp.mean(mixed_f * mixed_f, axis=1, keepdims=True)
    normed = (mixed_f * lax.rsqrt(square + 1e-06) * norm_gain[None, :]).astype(jnp.bfloat16)

    ids_all = lax.all_to_all(
        jnp.broadcast_to(expert_ids[None], (n_exp,) + expert_ids.shape),
        EXP,
        split_axis=0,
        concat_axis=0,
        tiled=True,
    ).reshape(n_exp * tok_dev, TOPK)
    cur = normed
    order = [0]
    for bit in doubling_bits(n_zl):
        other = lax.ppermute(cur, "zl", [(i, i ^ bit) for i in range(n_zl)])
        low = (zl_index & bit) == 0
        cur = jnp.where(low, jnp.concatenate([cur, other]), jnp.concatenate([other, cur]))
        order = order + [o + bit for o in order]
    partner = lax.ppermute(cur, "c", [(0, 1), (1, 0)])
    both = jnp.where(
        core_index == 0, jnp.concatenate([cur, partner]), jnp.concatenate([partner, cur])
    )
    blocks = []
    for src in range(n_exp):
        q = (src % 2) * n_zl + order.index(src // 2)
        blocks.append(both[q * tok_dev : (q + 1) * tok_dev])
    gathered = jnp.concatenate(blocks)
    normed_all = gathered

    most_slots = 3 * tok_dev // 4
    chosen = jnp.any(ids_all == exp_index, axis=1).astype(jnp.int32).reshape(n_exp, tok_dev)
    rank = jnp.cumsum(chosen, axis=1) - chosen
    dest = jnp.where(
        chosen == 1, jnp.arange(n_exp, dtype=jnp.int32)[:, None] * most_slots + rank, -1
    ).reshape(-1)
    placing = (
        jnp.arange(n_exp * most_slots, dtype=jnp.int32)[:, None] == dest[None, :]
    ).astype(jnp.bfloat16)
    received = jnp.dot(placing, normed_all, preferred_element_type=jnp.float32).astype(
        jnp.bfloat16
    )

    ids_flat = expert_ids.reshape(-1)
    onehot = (ids_flat[:, None] == jnp.arange(EXPERTS, dtype=jnp.int32)[None, :]).astype(jnp.int32)
    earlier = jnp.cumsum(onehot, axis=0) - onehot
    slot = jnp.sum(earlier * onehot, axis=1)
    target = ids_flat * most_slots + slot

    proj = jnp.einsum("sd,fd->sf", received, w_all, preferred_element_type=jnp.float32)
    proj = proj.reshape(EXPERTS * most_slots, n_xy, n_zh, 2, fe_dev)
    hidden = jax.nn.silu(proj[:, :, :, 0]) * proj[:, :, :, 1]
    hidden = jnp.transpose(hidden, (0, 2, 1, 3)).reshape(EXPERTS, most_slots, FE)
    returned = (
        lax.all_to_all(hidden.astype(jnp.bfloat16), EXP, split_axis=0, concat_axis=0, tiled=True)
        .astype(jnp.float32)
        .reshape(EXPERTS * most_slots, FE)
    )
    picked = jnp.take(returned, target, axis=0)
    routed = (picked * route_weight.reshape(-1)[:, None]).astype(jnp.bfloat16)
    return (mixed, routed.reshape(tok_dev, TOPK, FE))


def solution(mesh):
    n_ctx = mesh.shape["ctx"]
    n_exp = mesh.shape["exp"]
    n_zh = 2
    n_xy = n_ctx // n_zh
    side = int(round(math.sqrt(n_xy)))
    n_zl = n_exp // 2
    fine = Mesh(mesh.devices.reshape(n_zh, side, n_xy // side, n_zl, 2), CTX + EXP)
    tok = CTX + EXP
    in_specs = (
        P(tok, None),
        P(CTX, EXP),
        P(CTX, None),
        P(CTX, None),
        P(),
        P(EXP, None),
        P(),
        P(EXP, None, CTX),
        P(EXP, None, CTX),
        P(tok, None),
        P(tok, None),
    )
    out_specs = (P(tok, None), P(tok, None, None))

    def body(*args):
        return shards(*args, n_ctx=n_ctx, n_xy=n_xy, n_zh=n_zh)

    return jax.shard_map(body, mesh=fine, in_specs=in_specs, out_specs=out_specs, check_vma=False)
```

```python
import math

import jax
import jax.numpy as jnp
import numpy as np
from jax import lax
from jax.sharding import Mesh
from jax.sharding import PartitionSpec as P

D = 4096
HQ = 32
KVH = 2
HD = 128
FE = 768
EXPERTS = 16
TOPK = 8
CH = 64

CTX = ("zh", "x", "y")
EXP = ("zl", "c")


def stored_positions(span_pos, rows):
    span = rows // CH
    table = span[:, None] == jnp.arange(span_pos.shape[0], dtype=jnp.int32)[None, :]
    base = jnp.sum(jnp.where(table, span_pos[None, :], 0), axis=1)
    return base * CH + rows % CH


def doubling_bits(n):
    bits = []
    b = n // 2
    while b >= 1:
        bits.append(b)
        b //= 2
    return bits


def gather_by_doubling(piece, n):
    idx = lax.axis_index(CTX)
    cur = piece
    order = [0]
    for bit in doubling_bits(n):
        other = lax.ppermute(cur, CTX, [(i, i ^ bit) for i in range(n)])
        low = (idx & bit) == 0
        cur = jnp.where(low, jnp.concatenate([cur, other]), jnp.concatenate([other, cur]))
        order = order + [o + bit for o in order]
    return cur, order


def shards(
    residual,
    queries,
    keys,
    values,
    span_pos,
    out_proj,
    norm_gain,
    expert_gate,
    expert_up,
    expert_ids,
    route_weight,
    n_ctx,
    n_xy,
    n_zh,
):
    tok_rows = queries.shape[0]
    per_device = queries.shape[1] // HD
    group = HQ // KVH
    ctx_index = lax.axis_index(CTX)
    exp_index = lax.axis_index(EXP)
    n_exp = EXPERTS

    fe_dev = expert_gate.shape[2]
    w_local = jnp.concatenate([expert_gate[0].T, expert_up[0].T], axis=0)
    zh_index = lax.axis_index("zh")
    core_index = lax.axis_index("c")

    kv_head = exp_index * per_device // group
    own_keys = lax.dynamic_slice_in_dim(keys, kv_head * HD, HD, 1)
    own_values = lax.dynamic_slice_in_dim(values, kv_head * HD, HD, 1)
    kv_local = jnp.where(core_index == 0, own_keys, own_values)

    bits = doubling_bits(n_ctx)
    first = bits[0]
    kv_other = lax.ppermute(kv_local, CTX, [(i, i ^ first) for i in range(n_ctx)])
    w_other = lax.ppermute(w_local, "zh", [(0, 1), (1, 0)])
    w_pair = jnp.where(
        zh_index == 0,
        jnp.concatenate([w_local, w_other]),
        jnp.concatenate([w_other, w_local]),
    )
    w_all = lax.all_gather(w_pair, ("x", "y"), axis=0, tiled=True)

    low = (ctx_index & first) == 0
    cur = jnp.where(
        low, jnp.concatenate([kv_local, kv_other]), jnp.concatenate([kv_other, kv_local])
    )
    order = [0, first]
    for bit in bits[1:]:
        other = lax.ppermute(cur, CTX, [(i, i ^ bit) for i in range(n_ctx)])
        low = (ctx_index & bit) == 0
        cur = jnp.where(low, jnp.concatenate([cur, other]), jnp.concatenate([other, cur]))
        order = order + [o + bit for o in order]
    partner = lax.ppermute(cur, "c", [(0, 1), (1, 0)])
    key_piece = jnp.where(core_index == 0, cur, partner)
    value_piece = jnp.where(core_index == 0, partner, cur)
    length = key_piece.shape[0]
    block_ctx = jnp.asarray(np.array(order, np.int32))
    key_rows_all = (
        jnp.repeat(block_ctx, tok_rows) * tok_rows
        + jnp.tile(jnp.arange(tok_rows, dtype=jnp.int32), n_ctx)
    )

    query_pos = stored_positions(
        span_pos, ctx_index * tok_rows + jnp.arange(tok_rows, dtype=jnp.int32)
    )
    query_heads = queries.reshape(tok_rows, per_device, HD)
    scale = 1.0 / math.sqrt(HD)
    carry = (
        jnp.full((per_device, tok_rows), -1e30, jnp.float32),
        jnp.zeros((per_device, tok_rows), jnp.float32),
        jnp.zeros((per_device, tok_rows, HD), jnp.float32),
    )
    block = min(length, 1024)
    for begin in range(0, length, block):
        stop = min(begin + block, length)
        attend_key_piece = key_piece[begin:stop]
        attend_value_piece = value_piece[begin:stop]
        attend_running, attend_total, attend_accum = carry
        key_pos = stored_positions(span_pos, key_rows_all[begin:stop])
        scores = (
            jnp.einsum(
                "tqd,nd->qtn", query_heads, attend_key_piece, preferred_element_type=jnp.float32
            )
            * scale
        )
        visible = key_pos[None, None, :] <= query_pos[None, :, None]
        block_top = jnp.max(jnp.where(visible, scores, -1e30), axis=2)
        new_top = jnp.maximum(attend_running, block_top)
        factor = jnp.exp(attend_running - new_top)
        probs = jnp.where(visible, jnp.exp(scores - new_top[:, :, None]), 0.0)
        attend_total = attend_total * factor + jnp.sum(probs, axis=2)
        summed = jnp.einsum(
            "qtn,nd->qtd",
            probs.astype(jnp.bfloat16),
            attend_value_piece,
            preferred_element_type=jnp.float32,
        )
        attend_accum = attend_accum * factor[:, :, None] + summed
        carry = (new_top, attend_total, attend_accum)
    running, total, accum = carry
    attn = (accum / total[:, :, None]).astype(jnp.bfloat16)
    attn = jnp.transpose(attn, (1, 0, 2)).reshape(tok_rows, per_device * HD)
    tok_dev = residual.shape[0]

    share = jnp.dot(attn, out_proj, preferred_element_type=jnp.float32).astype(jnp.bfloat16)
    zl_index = lax.axis_index("zl")
    n_zl = n_exp // 2
    by_core = jnp.transpose(share.reshape(n_zl, 2, tok_dev, D), (1, 0, 2, 3))
    keep = jnp.where(core_index == 0, by_core[0], by_core[1])
    give = jnp.where(core_index == 0, by_core[1], by_core[0])
    got = lax.ppermute(give, "c", [(0, 1), (1, 0)])
    part = keep.astype(jnp.float32) + got.astype(jnp.float32)
    pair_sum = part.astype(jnp.bfloat16)
    shares = lax.all_to_all(pair_sum, "zl", split_axis=0, concat_axis=0, tiled=True)
    head_total = jnp.sum(shares.astype(jnp.float32), axis=0)
    mixed = (residual.astype(jnp.float32) + head_total).astype(jnp.bfloat16)
    mixed_f = mixed.astype(jnp.float32)
    square = jnp.mean(mixed_f * mixed_f, axis=1, keepdims=True)
    normed = (mixed_f * lax.rsqrt(square + 1e-06) * norm_gain[None, :]).astype(jnp.bfloat16)

    ids_all = lax.all_to_all(
        jnp.broadcast_to(expert_ids[None], (n_exp,) + expert_ids.shape),
        EXP,
        split_axis=0,
        concat_axis=0,
        tiled=True,
    ).reshape(n_exp * tok_dev, TOPK)
    cur = normed
    order = [0]
    for bit in doubling_bits(n_zl):
        other = lax.ppermute(cur, "zl", [(i, i ^ bit) for i in range(n_zl)])
        low = (zl_index & bit) == 0
        cur = jnp.where(low, jnp.concatenate([cur, other]), jnp.concatenate([other, cur]))
        order = order + [o + bit for o in order]
    partner = lax.ppermute(cur, "c", [(0, 1), (1, 0)])
    both = jnp.where(
        core_index == 0, jnp.concatenate([cur, partner]), jnp.concatenate([partner, cur])
    )
    blocks = []
    for src in range(n_exp):
        q = (src % 2) * n_zl + order.index(src // 2)
        blocks.append(both[q * tok_dev : (q + 1) * tok_dev])
    gathered = jnp.concatenate(blocks)
    normed_all = gathered

    most_slots = tok_dev
    chosen = jnp.any(ids_all == exp_index, axis=1).astype(jnp.int32).reshape(n_exp, tok_dev)
    rank = jnp.cumsum(chosen, axis=1) - chosen
    dest = jnp.where(
        chosen == 1, jnp.arange(n_exp, dtype=jnp.int32)[:, None] * most_slots + rank, -1
    ).reshape(-1)
    placing = (
        jnp.arange(n_exp * most_slots, dtype=jnp.int32)[:, None] == dest[None, :]
    ).astype(jnp.bfloat16)
    received = jnp.dot(placing, normed_all, preferred_element_type=jnp.float32).astype(
        jnp.bfloat16
    )

    ids_flat = expert_ids.reshape(-1)
    onehot = (ids_flat[:, None] == jnp.arange(EXPERTS, dtype=jnp.int32)[None, :]).astype(jnp.int32)
    earlier = jnp.cumsum(onehot, axis=0) - onehot
    slot = jnp.sum(earlier * onehot, axis=1)
    target = ids_flat * most_slots + slot

    proj = jnp.einsum("fd,sd->fs", w_all, received, preferred_element_type=jnp.float32)
    proj = proj.reshape(n_xy, n_zh, 2, fe_dev, EXPERTS * most_slots)
    hidden = jax.nn.silu(proj[:, :, 0]) * proj[:, :, 1]
    hidden = jnp.transpose(hidden, (1, 0, 2, 3)).reshape(FE, EXPERTS * most_slots)
    hidden = hidden.astype(jnp.bfloat16).T.reshape(EXPERTS, most_slots, FE)
    returned = (
        lax.all_to_all(hidden, EXP, split_axis=0, concat_axis=0, tiled=True)
        .astype(jnp.float32)
        .reshape(EXPERTS * most_slots, FE)
    )
    picked = jnp.take(returned, target, axis=0)
    routed = (picked * route_weight.reshape(-1)[:, None]).astype(jnp.bfloat16)
    return (mixed, routed.reshape(tok_dev, TOPK, FE))


def solution(mesh):
    n_ctx = mesh.shape["ctx"]
    n_exp = mesh.shape["exp"]
    n_zh = 2
    n_xy = n_ctx // n_zh
    side = int(round(math.sqrt(n_xy)))
    n_zl = n_exp // 2
    fine = Mesh(mesh.devices.reshape(n_zh, side, n_xy // side, n_zl, 2), CTX + EXP)
    tok = CTX + EXP
    in_specs = (
        P(tok, None),
        P(CTX, EXP),
        P(CTX, None),
        P(CTX, None),
        P(),
        P(EXP, None),
        P(),
        P(EXP, None, CTX),
        P(EXP, None, CTX),
        P(tok, None),
        P(tok, None),
    )
    out_specs = (P(tok, None), P(tok, None, None))

    def body(*args):
        return shards(*args, n_ctx=n_ctx, n_xy=n_xy, n_zh=n_zh)

    return jax.shard_map(body, mesh=fine, in_specs=in_specs, out_specs=out_specs, check_vma=False)
```

```python
import math

import jax
import jax.numpy as jnp
import numpy as np
from jax import lax
from jax.sharding import Mesh
from jax.sharding import PartitionSpec as P

D = 4096
HQ = 32
KVH = 2
HD = 128
FE = 768
EXPERTS = 16
TOPK = 8
CH = 64

CTX = ("zh", "x", "y")
EXP = ("zl", "c")


def stored_positions(span_pos, rows):
    span = rows // CH
    table = span[:, None] == jnp.arange(span_pos.shape[0], dtype=jnp.int32)[None, :]
    base = jnp.sum(jnp.where(table, span_pos[None, :], 0), axis=1)
    return base * CH + rows % CH


def doubling_bits(n):
    bits = []
    b = n // 2
    while b >= 1:
        bits.append(b)
        b //= 2
    return bits


def gather_by_doubling(piece, n):
    idx = lax.axis_index(CTX)
    cur = piece
    order = [0]
    for bit in doubling_bits(n):
        other = lax.ppermute(cur, CTX, [(i, i ^ bit) for i in range(n)])
        low = (idx & bit) == 0
        cur = jnp.where(low, jnp.concatenate([cur, other]), jnp.concatenate([other, cur]))
        order = order + [o + bit for o in order]
    return cur, order


def shards(
    residual,
    queries,
    keys,
    values,
    span_pos,
    out_proj,
    norm_gain,
    expert_gate,
    expert_up,
    expert_ids,
    route_weight,
    n_ctx,
    n_xy,
    n_zh,
):
    tok_rows = queries.shape[0]
    per_device = queries.shape[1] // HD
    group = HQ // KVH
    ctx_index = lax.axis_index(CTX)
    exp_index = lax.axis_index(EXP)
    n_exp = EXPERTS

    fe_dev = expert_gate.shape[2]
    w_local = jnp.concatenate([expert_gate[0].T, expert_up[0].T], axis=0)
    zh_index = lax.axis_index("zh")
    core_index = lax.axis_index("c")

    kv_head = exp_index * per_device // group
    own_keys = lax.dynamic_slice_in_dim(keys, kv_head * HD, HD, 1)
    own_values = lax.dynamic_slice_in_dim(values, kv_head * HD, HD, 1)
    kv_local = jnp.where(core_index == 0, own_keys, own_values)

    bits = doubling_bits(n_ctx)
    first = bits[0]
    kv_other = lax.ppermute(kv_local, CTX, [(i, i ^ first) for i in range(n_ctx)])
    w_other = lax.ppermute(w_local, "zh", [(0, 1), (1, 0)])
    w_pair = jnp.where(
        zh_index == 0,
        jnp.concatenate([w_local, w_other]),
        jnp.concatenate([w_other, w_local]),
    )
    w_all = lax.all_gather(w_pair, ("x", "y"), axis=0, tiled=True)

    low = (ctx_index & first) == 0
    cur = jnp.where(
        low, jnp.concatenate([kv_local, kv_other]), jnp.concatenate([kv_other, kv_local])
    )
    order = [0, first]
    for bit in bits[1:]:
        other = lax.ppermute(cur, CTX, [(i, i ^ bit) for i in range(n_ctx)])
        low = (ctx_index & bit) == 0
        cur = jnp.where(low, jnp.concatenate([cur, other]), jnp.concatenate([other, cur]))
        order = order + [o + bit for o in order]
    partner = lax.ppermute(cur, "c", [(0, 1), (1, 0)])
    key_piece = jnp.where(core_index == 0, cur, partner)
    value_piece = jnp.where(core_index == 0, partner, cur)
    length = key_piece.shape[0]
    block_ctx = jnp.asarray(np.array(order, np.int32))
    key_rows_all = (
        jnp.repeat(block_ctx, tok_rows) * tok_rows
        + jnp.tile(jnp.arange(tok_rows, dtype=jnp.int32), n_ctx)
    )

    query_pos = stored_positions(
        span_pos, ctx_index * tok_rows + jnp.arange(tok_rows, dtype=jnp.int32)
    )
    query_heads = queries.reshape(tok_rows, per_device, HD)
    scale = 1.0 / math.sqrt(HD)
    carry = (
        jnp.full((per_device, tok_rows), -1e30, jnp.float32),
        jnp.zeros((per_device, tok_rows), jnp.float32),
        jnp.zeros((per_device, tok_rows, HD), jnp.float32),
    )
    block = min(length, 1024)
    for begin in range(0, length, block):
        stop = min(begin + block, length)
        attend_key_piece = key_piece[begin:stop]
        attend_value_piece = value_piece[begin:stop]
        attend_running, attend_total, attend_accum = carry
        key_pos = stored_positions(span_pos, key_rows_all[begin:stop])
        scores = (
            jnp.einsum(
                "tqd,nd->qtn", query_heads, attend_key_piece, preferred_element_type=jnp.float32
            )
            * scale
        )
        visible = key_pos[None, None, :] <= query_pos[None, :, None]
        block_top = jnp.max(jnp.where(visible, scores, -1e30), axis=2)
        new_top = jnp.maximum(attend_running, block_top)
        factor = jnp.exp(attend_running - new_top)
        probs = jnp.where(visible, jnp.exp(scores - new_top[:, :, None]), 0.0)
        attend_total = attend_total * factor + jnp.sum(probs, axis=2)
        summed = jnp.einsum(
            "qtn,nd->qtd",
            probs.astype(jnp.bfloat16),
            attend_value_piece,
            preferred_element_type=jnp.float32,
        )
        attend_accum = attend_accum * factor[:, :, None] + summed
        carry = (new_top, attend_total, attend_accum)
    running, total, accum = carry
    attn = (accum / total[:, :, None]).astype(jnp.bfloat16)
    attn = jnp.transpose(attn, (1, 0, 2)).reshape(tok_rows, per_device * HD)
    tok_dev = residual.shape[0]

    share = jnp.dot(attn, out_proj, preferred_element_type=jnp.float32).astype(jnp.bfloat16)
    zl_index = lax.axis_index("zl")
    n_zl = n_exp // 2
    by_core = jnp.transpose(share.reshape(n_zl, 2, tok_dev, D), (1, 0, 2, 3))
    keep = jnp.where(core_index == 0, by_core[0], by_core[1])
    give = jnp.where(core_index == 0, by_core[1], by_core[0])
    got = lax.ppermute(give, "c", [(0, 1), (1, 0)])
    part = keep.astype(jnp.float32) + got.astype(jnp.float32)
    pair_sum = part.astype(jnp.bfloat16)
    shares = lax.all_to_all(pair_sum, "zl", split_axis=0, concat_axis=0, tiled=True)
    head_total = jnp.sum(shares.astype(jnp.float32), axis=0)
    mixed = (residual.astype(jnp.float32) + head_total).astype(jnp.bfloat16)
    mixed_f = mixed.astype(jnp.float32)
    square = jnp.mean(mixed_f * mixed_f, axis=1, keepdims=True)
    normed = (mixed_f * lax.rsqrt(square + 1e-06) * norm_gain[None, :]).astype(jnp.bfloat16)

    ids_all = lax.all_to_all(
        jnp.broadcast_to(expert_ids[None], (n_exp,) + expert_ids.shape),
        EXP,
        split_axis=0,
        concat_axis=0,
        tiled=True,
    ).reshape(n_exp * tok_dev, TOPK)
    cur = normed
    order = [0]
    for bit in doubling_bits(n_zl):
        other = lax.ppermute(cur, "zl", [(i, i ^ bit) for i in range(n_zl)])
        low = (zl_index & bit) == 0
        cur = jnp.where(low, jnp.concatenate([cur, other]), jnp.concatenate([other, cur]))
        order = order + [o + bit for o in order]
    partner = lax.ppermute(cur, "c", [(0, 1), (1, 0)])
    both = jnp.where(
        core_index == 0, jnp.concatenate([cur, partner]), jnp.concatenate([partner, cur])
    )
    blocks = []
    for src in range(n_exp):
        q = (src % 2) * n_zl + order.index(src // 2)
        blocks.append(both[q * tok_dev : (q + 1) * tok_dev])
    gathered = jnp.concatenate(blocks)
    normed_all = gathered

    most_slots = tok_dev
    chosen = jnp.any(ids_all == exp_index, axis=1).astype(jnp.int32).reshape(n_exp, tok_dev)
    rank = jnp.cumsum(chosen, axis=1) - chosen
    dest = jnp.where(
        chosen == 1, jnp.arange(n_exp, dtype=jnp.int32)[:, None] * most_slots + rank, -1
    ).reshape(-1)
    placing = (
        jnp.arange(n_exp * most_slots, dtype=jnp.int32)[:, None] == dest[None, :]
    ).astype(jnp.bfloat16)
    received = jnp.dot(placing, normed_all, preferred_element_type=jnp.float32).astype(
        jnp.bfloat16
    )
    received = lax.optimization_barrier(received)

    ids_flat = expert_ids.reshape(-1)
    onehot = (ids_flat[:, None] == jnp.arange(EXPERTS, dtype=jnp.int32)[None, :]).astype(jnp.int32)
    earlier = jnp.cumsum(onehot, axis=0) - onehot
    slot = jnp.sum(earlier * onehot, axis=1)
    target = ids_flat * most_slots + slot

    proj = jnp.einsum("fd,sd->fs", w_all, received, preferred_element_type=jnp.float32)
    proj = proj.reshape(n_xy, n_zh, 2, fe_dev, EXPERTS * most_slots)
    hidden = jax.nn.silu(proj[:, :, 0]) * proj[:, :, 1]
    hidden = jnp.transpose(hidden, (1, 0, 2, 3)).reshape(FE, EXPERTS * most_slots)
    hidden = hidden.astype(jnp.bfloat16).T.reshape(EXPERTS, most_slots, FE)
    returned = (
        lax.all_to_all(hidden, EXP, split_axis=0, concat_axis=0, tiled=True)
        .astype(jnp.float32)
        .reshape(EXPERTS * most_slots, FE)
    )
    picked = jnp.take(returned, target, axis=0)
    routed = (picked * route_weight.reshape(-1)[:, None]).astype(jnp.bfloat16)
    return (mixed, routed.reshape(tok_dev, TOPK, FE))


def solution(mesh):
    n_ctx = mesh.shape["ctx"]
    n_exp = mesh.shape["exp"]
    n_zh = 2
    n_xy = n_ctx // n_zh
    side = int(round(math.sqrt(n_xy)))
    n_zl = n_exp // 2
    fine = Mesh(mesh.devices.reshape(n_zh, side, n_xy // side, n_zl, 2), CTX + EXP)
    tok = CTX + EXP
    in_specs = (
        P(tok, None),
        P(CTX, EXP),
        P(CTX, None),
        P(CTX, None),
        P(),
        P(EXP, None),
        P(),
        P(EXP, None, CTX),
        P(EXP, None, CTX),
        P(tok, None),
        P(tok, None),
    )
    out_specs = (P(tok, None), P(tok, None, None))

    def body(*args):
        return shards(*args, n_ctx=n_ctx, n_xy=n_xy, n_zh=n_zh)

    return jax.shard_map(body, mesh=fine, in_specs=in_specs, out_specs=out_specs, check_vma=False)
```

```python
import math

import jax
import jax.numpy as jnp
import numpy as np
from jax import lax
from jax.sharding import Mesh
from jax.sharding import PartitionSpec as P

D = 4096
HQ = 32
KVH = 2
HD = 128
FE = 768
EXPERTS = 16
TOPK = 8
CH = 64

CTX = ("zh", "x", "y")
EXP = ("zl", "c")


def stored_positions(span_pos, rows):
    span = rows // CH
    table = span[:, None] == jnp.arange(span_pos.shape[0], dtype=jnp.int32)[None, :]
    base = jnp.sum(jnp.where(table, span_pos[None, :], 0), axis=1)
    return base * CH + rows % CH


def doubling_bits(n):
    bits = []
    b = n // 2
    while b >= 1:
        bits.append(b)
        b //= 2
    return bits


def gather_by_doubling(piece, n):
    idx = lax.axis_index(CTX)
    cur = piece
    order = [0]
    for bit in doubling_bits(n):
        other = lax.ppermute(cur, CTX, [(i, i ^ bit) for i in range(n)])
        low = (idx & bit) == 0
        cur = jnp.where(low, jnp.concatenate([cur, other]), jnp.concatenate([other, cur]))
        order = order + [o + bit for o in order]
    return cur, order


def shards(
    residual,
    queries,
    keys,
    values,
    span_pos,
    out_proj,
    norm_gain,
    expert_gate,
    expert_up,
    expert_ids,
    route_weight,
    n_ctx,
    n_xy,
    n_zh,
):
    tok_rows = queries.shape[0]
    per_device = queries.shape[1] // HD
    group = HQ // KVH
    ctx_index = lax.axis_index(CTX)
    exp_index = lax.axis_index(EXP)
    n_exp = EXPERTS

    fe_dev = expert_gate.shape[2]
    w_local = jnp.concatenate([expert_gate[0].T, expert_up[0].T], axis=0)
    zh_index = lax.axis_index("zh")
    core_index = lax.axis_index("c")

    kv_head = exp_index * per_device // group
    own_keys = lax.dynamic_slice_in_dim(keys, kv_head * HD, HD, 1)
    own_values = lax.dynamic_slice_in_dim(values, kv_head * HD, HD, 1)
    kv_local = jnp.where(core_index == 0, own_keys, own_values)

    bits = doubling_bits(n_ctx)
    first = bits[0]
    kv_other = lax.ppermute(kv_local, CTX, [(i, i ^ first) for i in range(n_ctx)])
    w_other = lax.ppermute(w_local, "zh", [(0, 1), (1, 0)])
    w_pair = jnp.where(
        zh_index == 0,
        jnp.concatenate([w_local, w_other]),
        jnp.concatenate([w_other, w_local]),
    )
    w_all = lax.all_gather(w_pair, ("x", "y"), axis=0, tiled=True)

    low = (ctx_index & first) == 0
    cur = jnp.where(
        low, jnp.concatenate([kv_local, kv_other]), jnp.concatenate([kv_other, kv_local])
    )
    order = [0, first]
    for step, bit in enumerate(bits[1:]):
        other = lax.ppermute(cur, CTX, [(i, i ^ bit) for i in range(n_ctx)])
        low = (ctx_index & bit) == 0
        cur = jnp.where(low, jnp.concatenate([cur, other]), jnp.concatenate([other, cur]))
        order = order + [o + bit for o in order]
        if step == 2:
            w_pair, cur = lax.optimization_barrier((w_pair, cur))
    partner = lax.ppermute(cur, "c", [(0, 1), (1, 0)])
    key_piece = jnp.where(core_index == 0, cur, partner)
    value_piece = jnp.where(core_index == 0, partner, cur)
    length = key_piece.shape[0]
    block_ctx = jnp.asarray(np.array(order, np.int32))
    key_rows_all = (
        jnp.repeat(block_ctx, tok_rows) * tok_rows
        + jnp.tile(jnp.arange(tok_rows, dtype=jnp.int32), n_ctx)
    )

    query_pos = stored_positions(
        span_pos, ctx_index * tok_rows + jnp.arange(tok_rows, dtype=jnp.int32)
    )
    query_heads = queries.reshape(tok_rows, per_device, HD)
    scale = 1.0 / math.sqrt(HD)
    carry = (
        jnp.full((per_device, tok_rows), -1e30, jnp.float32),
        jnp.zeros((per_device, tok_rows), jnp.float32),
        jnp.zeros((per_device, tok_rows, HD), jnp.float32),
    )
    block = min(length, 1024)
    for begin in range(0, length, block):
        stop = min(begin + block, length)
        attend_key_piece = key_piece[begin:stop]
        attend_value_piece = value_piece[begin:stop]
        attend_running, attend_total, attend_accum = carry
        key_pos = stored_positions(span_pos, key_rows_all[begin:stop])
        scores = (
            jnp.einsum(
                "tqd,nd->qtn", query_heads, attend_key_piece, preferred_element_type=jnp.float32
            )
            * scale
        )
        visible = key_pos[None, None, :] <= query_pos[None, :, None]
        block_top = jnp.max(jnp.where(visible, scores, -1e30), axis=2)
        new_top = jnp.maximum(attend_running, block_top)
        factor = jnp.exp(attend_running - new_top)
        probs = jnp.where(visible, jnp.exp(scores - new_top[:, :, None]), 0.0)
        attend_total = attend_total * factor + jnp.sum(probs, axis=2)
        summed = jnp.einsum(
            "qtn,nd->qtd",
            probs.astype(jnp.bfloat16),
            attend_value_piece,
            preferred_element_type=jnp.float32,
        )
        attend_accum = attend_accum * factor[:, :, None] + summed
        carry = (new_top, attend_total, attend_accum)
    running, total, accum = carry
    attn = (accum / total[:, :, None]).astype(jnp.bfloat16)
    attn = jnp.transpose(attn, (1, 0, 2)).reshape(tok_rows, per_device * HD)
    tok_dev = residual.shape[0]

    share = jnp.dot(attn, out_proj, preferred_element_type=jnp.float32).astype(jnp.bfloat16)
    zl_index = lax.axis_index("zl")
    n_zl = n_exp // 2
    by_core = jnp.transpose(share.reshape(n_zl, 2, tok_dev, D), (1, 0, 2, 3))
    keep = jnp.where(core_index == 0, by_core[0], by_core[1])
    give = jnp.where(core_index == 0, by_core[1], by_core[0])
    got = lax.ppermute(give, "c", [(0, 1), (1, 0)])
    part = keep.astype(jnp.float32) + got.astype(jnp.float32)
    pair_sum = part.astype(jnp.bfloat16)
    shares = lax.all_to_all(pair_sum, "zl", split_axis=0, concat_axis=0, tiled=True)
    head_total = jnp.sum(shares.astype(jnp.float32), axis=0)
    mixed = (residual.astype(jnp.float32) + head_total).astype(jnp.bfloat16)
    mixed_f = mixed.astype(jnp.float32)
    square = jnp.mean(mixed_f * mixed_f, axis=1, keepdims=True)
    normed = (mixed_f * lax.rsqrt(square + 1e-06) * norm_gain[None, :]).astype(jnp.bfloat16)

    ids_all = lax.all_to_all(
        jnp.broadcast_to(expert_ids[None], (n_exp,) + expert_ids.shape),
        EXP,
        split_axis=0,
        concat_axis=0,
        tiled=True,
    ).reshape(n_exp * tok_dev, TOPK)
    cur = normed
    order = [0]
    for bit in doubling_bits(n_zl):
        other = lax.ppermute(cur, "zl", [(i, i ^ bit) for i in range(n_zl)])
        low = (zl_index & bit) == 0
        cur = jnp.where(low, jnp.concatenate([cur, other]), jnp.concatenate([other, cur]))
        order = order + [o + bit for o in order]
    partner = lax.ppermute(cur, "c", [(0, 1), (1, 0)])
    both = jnp.where(
        core_index == 0, jnp.concatenate([cur, partner]), jnp.concatenate([partner, cur])
    )
    blocks = []
    for src in range(n_exp):
        q = (src % 2) * n_zl + order.index(src // 2)
        blocks.append(both[q * tok_dev : (q + 1) * tok_dev])
    gathered = jnp.concatenate(blocks)
    normed_all = gathered

    most_slots = tok_dev
    chosen = jnp.any(ids_all == exp_index, axis=1).astype(jnp.int32).reshape(n_exp, tok_dev)
    rank = jnp.cumsum(chosen, axis=1) - chosen
    dest = jnp.where(
        chosen == 1, jnp.arange(n_exp, dtype=jnp.int32)[:, None] * most_slots + rank, -1
    ).reshape(-1)
    placing = (
        jnp.arange(n_exp * most_slots, dtype=jnp.int32)[:, None] == dest[None, :]
    ).astype(jnp.bfloat16)
    received = jnp.dot(placing, normed_all, preferred_element_type=jnp.float32).astype(
        jnp.bfloat16
    )
    received = lax.optimization_barrier(received)

    ids_flat = expert_ids.reshape(-1)
    onehot = (ids_flat[:, None] == jnp.arange(EXPERTS, dtype=jnp.int32)[None, :]).astype(jnp.int32)
    earlier = jnp.cumsum(onehot, axis=0) - onehot
    slot = jnp.sum(earlier * onehot, axis=1)
    target = ids_flat * most_slots + slot

    proj = jnp.einsum("fd,sd->fs", w_all, received, preferred_element_type=jnp.float32)
    proj = proj.reshape(n_xy, n_zh, 2, fe_dev, EXPERTS * most_slots)
    hidden = jax.nn.silu(proj[:, :, 0]) * proj[:, :, 1]
    hidden = jnp.transpose(hidden, (1, 0, 2, 3)).reshape(FE, EXPERTS * most_slots)
    hidden = hidden.astype(jnp.bfloat16).T.reshape(EXPERTS, most_slots, FE)
    returned = (
        lax.all_to_all(hidden, EXP, split_axis=0, concat_axis=0, tiled=True)
        .astype(jnp.float32)
        .reshape(EXPERTS * most_slots, FE)
    )
    picked = jnp.take(returned, target, axis=0)
    routed = (picked * route_weight.reshape(-1)[:, None]).astype(jnp.bfloat16)
    return (mixed, routed.reshape(tok_dev, TOPK, FE))


def solution(mesh):
    n_ctx = mesh.shape["ctx"]
    n_exp = mesh.shape["exp"]
    n_zh = 2
    n_xy = n_ctx // n_zh
    side = int(round(math.sqrt(n_xy)))
    n_zl = n_exp // 2
    fine = Mesh(mesh.devices.reshape(n_zh, side, n_xy // side, n_zl, 2), CTX + EXP)
    tok = CTX + EXP
    in_specs = (
        P(tok, None),
        P(CTX, EXP),
        P(CTX, None),
        P(CTX, None),
        P(),
        P(EXP, None),
        P(),
        P(EXP, None, CTX),
        P(EXP, None, CTX),
        P(tok, None),
        P(tok, None),
    )
    out_specs = (P(tok, None), P(tok, None, None))

    def body(*args):
        return shards(*args, n_ctx=n_ctx, n_xy=n_xy, n_zh=n_zh)

    return jax.shard_map(body, mesh=fine, in_specs=in_specs, out_specs=out_specs, check_vma=False)
```

```python
import math

import jax
import jax.numpy as jnp
import numpy as np
from jax import lax
from jax.sharding import Mesh
from jax.sharding import PartitionSpec as P

D = 4096
HQ = 32
KVH = 2
HD = 128
FE = 768
EXPERTS = 16
TOPK = 8
CH = 64

CTX = ("zh", "x", "y")
EXP = ("zl", "c")


def stored_positions(span_pos, rows):
    span = rows // CH
    table = span[:, None] == jnp.arange(span_pos.shape[0], dtype=jnp.int32)[None, :]
    base = jnp.sum(jnp.where(table, span_pos[None, :], 0), axis=1)
    return base * CH + rows % CH


def doubling_bits(n):
    bits = []
    b = n // 2
    while b >= 1:
        bits.append(b)
        b //= 2
    return bits


def gather_by_doubling(piece, n):
    idx = lax.axis_index(CTX)
    cur = piece
    order = [0]
    for bit in doubling_bits(n):
        other = lax.ppermute(cur, CTX, [(i, i ^ bit) for i in range(n)])
        low = (idx & bit) == 0
        cur = jnp.where(low, jnp.concatenate([cur, other]), jnp.concatenate([other, cur]))
        order = order + [o + bit for o in order]
    return cur, order


def shards(
    residual,
    queries,
    keys,
    values,
    span_pos,
    out_proj,
    norm_gain,
    expert_gate,
    expert_up,
    expert_ids,
    route_weight,
    n_ctx,
    n_xy,
    n_zh,
):
    tok_rows = queries.shape[0]
    per_device = queries.shape[1] // HD
    group = HQ // KVH
    ctx_index = lax.axis_index(CTX)
    exp_index = lax.axis_index(EXP)
    n_exp = EXPERTS

    fe_dev = expert_gate.shape[2]
    w_local = jnp.concatenate([expert_gate[0].T, expert_up[0].T], axis=0)
    zh_index = lax.axis_index("zh")
    core_index = lax.axis_index("c")

    kv_head = exp_index * per_device // group
    own_keys = lax.dynamic_slice_in_dim(keys, kv_head * HD, HD, 1)
    own_values = lax.dynamic_slice_in_dim(values, kv_head * HD, HD, 1)
    kv_local = jnp.where(core_index == 0, own_keys, own_values)

    bits = doubling_bits(n_ctx)
    first = bits[0]
    kv_other = lax.ppermute(kv_local, CTX, [(i, i ^ first) for i in range(n_ctx)])
    w_other = lax.ppermute(w_local, "zh", [(0, 1), (1, 0)])
    w_pair = jnp.where(
        zh_index == 0,
        jnp.concatenate([w_local, w_other]),
        jnp.concatenate([w_other, w_local]),
    )
    w_all = lax.all_gather(w_pair, ("x", "y"), axis=0, tiled=True)

    low = (ctx_index & first) == 0
    cur = jnp.where(
        low, jnp.concatenate([kv_local, kv_other]), jnp.concatenate([kv_other, kv_local])
    )
    order = [0, first]
    for bit in bits[1:]:
        other = lax.ppermute(cur, CTX, [(i, i ^ bit) for i in range(n_ctx)])
        low = (ctx_index & bit) == 0
        cur = jnp.where(low, jnp.concatenate([cur, other]), jnp.concatenate([other, cur]))
        order = order + [o + bit for o in order]
    partner = lax.ppermute(cur, "c", [(0, 1), (1, 0)])
    key_piece = jnp.where(core_index == 0, cur, partner)
    value_piece = jnp.where(core_index == 0, partner, cur)
    length = key_piece.shape[0]
    block_ctx = jnp.asarray(np.array(order, np.int32))
    key_rows_all = (
        jnp.repeat(block_ctx, tok_rows) * tok_rows
        + jnp.tile(jnp.arange(tok_rows, dtype=jnp.int32), n_ctx)
    )

    query_pos = stored_positions(
        span_pos, ctx_index * tok_rows + jnp.arange(tok_rows, dtype=jnp.int32)
    )
    query_heads = queries.reshape(tok_rows, per_device, HD)
    scale = 1.0 / math.sqrt(HD)
    carry = (
        jnp.full((per_device, tok_rows), -1e30, jnp.float32),
        jnp.zeros((per_device, tok_rows), jnp.float32),
        jnp.zeros((per_device, tok_rows, HD), jnp.float32),
    )
    block = min(length, 1024)
    for begin in range(0, length, block):
        stop = min(begin + block, length)
        attend_key_piece = key_piece[begin:stop]
        attend_value_piece = value_piece[begin:stop]
        attend_running, attend_total, attend_accum = carry
        key_pos = stored_positions(span_pos, key_rows_all[begin:stop])
        scores = (
            jnp.einsum(
                "tqd,nd->qtn", query_heads, attend_key_piece, preferred_element_type=jnp.float32
            )
            * scale
        )
        visible = key_pos[None, None, :] <= query_pos[None, :, None]
        block_top = jnp.max(jnp.where(visible, scores, -1e30), axis=2)
        new_top = jnp.maximum(attend_running, block_top)
        factor = jnp.exp(attend_running - new_top)
        probs = jnp.where(visible, jnp.exp(scores - new_top[:, :, None]), 0.0)
        attend_total = attend_total * factor + jnp.sum(probs, axis=2)
        summed = jnp.einsum(
            "qtn,nd->qtd",
            probs.astype(jnp.bfloat16),
            attend_value_piece,
            preferred_element_type=jnp.float32,
        )
        attend_accum = attend_accum * factor[:, :, None] + summed
        carry = (new_top, attend_total, attend_accum)
    running, total, accum = carry
    attn = (accum / total[:, :, None]).astype(jnp.bfloat16)
    attn = jnp.transpose(attn, (1, 0, 2)).reshape(tok_rows, per_device * HD)
    tok_dev = residual.shape[0]

    share = jnp.dot(attn, out_proj, preferred_element_type=jnp.float32).astype(jnp.bfloat16)
    zl_index = lax.axis_index("zl")
    n_zl = n_exp // 2
    by_core = jnp.transpose(share.reshape(n_zl, 2, tok_dev, D), (1, 0, 2, 3))
    keep = jnp.where(core_index == 0, by_core[0], by_core[1])
    give = jnp.where(core_index == 0, by_core[1], by_core[0])
    got = lax.ppermute(give, "c", [(0, 1), (1, 0)])
    part = keep.astype(jnp.float32) + got.astype(jnp.float32)
    pair_sum = part.astype(jnp.bfloat16)
    shares = lax.all_to_all(pair_sum, "zl", split_axis=0, concat_axis=0, tiled=True)
    head_total = jnp.sum(shares.astype(jnp.float32), axis=0)
    mixed = (residual.astype(jnp.float32) + head_total).astype(jnp.bfloat16)
    mixed_f = mixed.astype(jnp.float32)
    square = jnp.mean(mixed_f * mixed_f, axis=1, keepdims=True)
    normed = (mixed_f * lax.rsqrt(square + 1e-06) * norm_gain[None, :]).astype(jnp.bfloat16)

    ids_rw = jnp.concatenate([expert_ids.astype(jnp.float32), route_weight], axis=1)
    ids_rw_all = lax.all_to_all(
        jnp.broadcast_to(ids_rw[None], (n_exp,) + ids_rw.shape),
        EXP,
        split_axis=0,
        concat_axis=0,
        tiled=True,
    ).reshape(n_exp * tok_dev, 2 * TOPK)
    ids_all = ids_rw_all[:, :TOPK].astype(jnp.int32)
    rw_all = ids_rw_all[:, TOPK:]
    cur = normed
    order = [0]
    for bit in doubling_bits(n_zl):
        other = lax.ppermute(cur, "zl", [(i, i ^ bit) for i in range(n_zl)])
        low = (zl_index & bit) == 0
        cur = jnp.where(low, jnp.concatenate([cur, other]), jnp.concatenate([other, cur]))
        order = order + [o + bit for o in order]
    partner = lax.ppermute(cur, "c", [(0, 1), (1, 0)])
    both = jnp.where(
        core_index == 0, jnp.concatenate([cur, partner]), jnp.concatenate([partner, cur])
    )
    blocks = []
    for src in range(n_exp):
        q = (src % 2) * n_zl + order.index(src // 2)
        blocks.append(both[q * tok_dev : (q + 1) * tok_dev])
    gathered = jnp.concatenate(blocks)
    normed_all = gathered

    most_slots = tok_dev
    chosen = jnp.any(ids_all == exp_index, axis=1).astype(jnp.int32).reshape(n_exp, tok_dev)
    rank = jnp.cumsum(chosen, axis=1) - chosen
    dest = jnp.where(
        chosen == 1, jnp.arange(n_exp, dtype=jnp.int32)[:, None] * most_slots + rank, -1
    ).reshape(-1)
    slot_of = jnp.arange(n_exp * most_slots, dtype=jnp.int32)[:, None] == dest[None, :]
    placing = slot_of.astype(jnp.bfloat16)
    rw_tok = jnp.sum(jnp.where(ids_all == exp_index, rw_all, 0.0), axis=1)
    rw_slot = jnp.sum(jnp.where(slot_of, rw_tok[None, :], 0.0), axis=1)
    received = jnp.dot(placing, normed_all, preferred_element_type=jnp.float32).astype(
        jnp.bfloat16
    )
    received = lax.optimization_barrier(received)

    ids_flat = expert_ids.reshape(-1)
    onehot = (ids_flat[:, None] == jnp.arange(EXPERTS, dtype=jnp.int32)[None, :]).astype(jnp.int32)
    earlier = jnp.cumsum(onehot, axis=0) - onehot
    slot = jnp.sum(earlier * onehot, axis=1)
    target = ids_flat * most_slots + slot

    proj = jnp.einsum("fd,sd->fs", w_all, received, preferred_element_type=jnp.float32)
    proj = proj.reshape(n_xy, n_zh, 2, fe_dev, EXPERTS * most_slots)
    hidden = jax.nn.silu(proj[:, :, 0]) * proj[:, :, 1]
    hidden = jnp.transpose(hidden, (1, 0, 2, 3)).reshape(FE, EXPERTS * most_slots)
    hidden = (hidden * rw_slot[None, :]).astype(jnp.bfloat16).T.reshape(EXPERTS, most_slots, FE)
    returned = lax.all_to_all(hidden, EXP, split_axis=0, concat_axis=0, tiled=True).reshape(
        EXPERTS * most_slots, FE
    )
    routed = jnp.take(returned, target, axis=0)
    return (mixed, routed.reshape(tok_dev, TOPK, FE))


def solution(mesh):
    n_ctx = mesh.shape["ctx"]
    n_exp = mesh.shape["exp"]
    n_zh = 2
    n_xy = n_ctx // n_zh
    side = int(round(math.sqrt(n_xy)))
    n_zl = n_exp // 2
    fine = Mesh(mesh.devices.reshape(n_zh, side, n_xy // side, n_zl, 2), CTX + EXP)
    tok = CTX + EXP
    in_specs = (
        P(tok, None),
        P(CTX, EXP),
        P(CTX, None),
        P(CTX, None),
        P(),
        P(EXP, None),
        P(),
        P(EXP, None, CTX),
        P(EXP, None, CTX),
        P(tok, None),
        P(tok, None),
    )
    out_specs = (P(tok, None), P(tok, None, None))

    def body(*args):
        return shards(*args, n_ctx=n_ctx, n_xy=n_xy, n_zh=n_zh)

    return jax.shard_map(body, mesh=fine, in_specs=in_specs, out_specs=out_specs, check_vma=False)
```
